512 devices in a mesh: fsdp: 64 (over z, x), sp: 8 (over y, core).
Axes of the slice: x: 4, y: 4, z: 16, core: 2. Of those that a mesh axis runs over, the one named last changes fastest.
Arguments:
- queries: bfloat16 [65536, 2048], P(('fsdp', 'sp')), may hold values from -6.5 to 6.5
- key_rows: bfloat16 [65536, 512], P(('fsdp', 'sp')), may hold values from -6.5 to 6.5
- value_rows: bfloat16 [65536, 512], P(('fsdp', 'sp')), may hold values from -6 to 6
- out_grad: bfloat16 [65536, 2048], P(('fsdp', 'sp')), may hold values from -6 to 6
- doc_lengths: int32 [128], replicated, may hold values from 1 to 16, 512 in all
Outputs:
- attn_out: bfloat16 [65536, 2048], P(('fsdp', 'sp'))
- grad_queries: bfloat16 [65536, 2048], P(('fsdp', 'sp'))
- grad_keys: bfloat16 [65536, 512], P(('fsdp', 'sp'))
- grad_values: bfloat16 [65536, 512], P(('fsdp', 'sp'))
The draws below stay inside these ranges and needn't reach their ends.
Inputs may be any that keep to these rules, and one draw needn't show every extreme that they name: Document d covers doc_lengths[d] blocks of 128 tokens right after documents 0 to d - 1; the lengths sum to 512 blocks.
All inputs are finite; a program needn't handle non-finite values.
Results may differ from the reference program's by a relative error of at most 0.012.
The reference program's roundings to bfloat16 on the way count: a program that leaves them out, or rounds other values in their place, can miss the bound.
Values may be sent and summed in bfloat16 or wider, within the bound.
No kernel may reach another device: no remote copies, remote signals or barrier semaphores. Data moves between devices by JAX's collectives and lax.ppermute only.
A program may use at most 64 MiB of HBM per device.

```python
import math
import jax
import jax.numpy as jnp
import numpy as np
from jax import lax

HQ = 16
KV = 4
HD = 128
BLK = 128
MOST_BLK = 16
TOKENS = 65536
NBLK = 512
NDOC = 128


def draw_queries(key, part):
    group_size = HQ // KV
    shape_full = (TOKENS, KV, group_size, HD)
    base_rows = jnp.clip(jax.random.normal(jax.random.fold_in(key, 1), shape_full, jnp.float32), -6.0, 6.0)
    return base_rows.reshape(TOKENS, HQ * HD).astype(jnp.bfloat16)


def draw_key_rows(key, part):
    shape_full = (TOKENS, KV, HD)
    base_rows = jnp.clip(jax.random.normal(jax.random.fold_in(key, 2), shape_full, jnp.float32), -6.0, 6.0)
    return base_rows.reshape(TOKENS, KV * HD).astype(jnp.bfloat16)


def level_of(stream_key, extent, shards, smallest, top_value):
    def one(dim, parts):
        draws = jax.random.uniform(jax.random.fold_in(jax.random.fold_in(stream_key, 6), dim), (parts,), jnp.float32, smallest / len(shards), top_value / len(shards))
        return jnp.repeat(jnp.exp(draws), extent[dim] // parts).reshape((-1,) + (1,) * (len(extent) - dim - 1))

    level = one(*shards[0])
    for cut in shards[1:]:
        level = level * one(*cut)
    return level


def split_up(count, total, most, lean):
    weights = [(1 << 20) // math.isqrt(standing ** lean) + 1 for standing in range(2, count + 1)]
    surplus, given = total - most - (count - 1), [1] * (count - 1)
    while surplus > 0:
        free = [i for i in range(count - 1) if given[i] < most]
        whole, budget = sum([weights[i] for i in free]), surplus
        for i in free:
            more = min(most - given[i], max(1, budget * weights[i] // whole), surplus)
            given[i] = given[i] + more
            surplus = surplus - more
    return np.array([most] + given)


def ragged(own_key, amount, total, reach, slope):
    if amount == 2:
        one = jax.random.randint(own_key, (), max(1, total - reach), min(reach, total - 1) + 1)
        return jnp.stack([one, total - one])
    tallies = jnp.asarray(split_up(amount, total, reach, slope), jnp.int32)
    twos = (amount - 1) // 2
    giver, receiver = tallies[1:1 + 2 * twos:2], tallies[2:2 + 2 * twos:2]
    slack = jnp.minimum(giver - 1, reach - receiver)
    passed = jax.random.randint(jax.random.fold_in(own_key, 1), (twos,), 0, 1 << 20) % (slack + 1)
    tallies = tallies.at[1:1 + 2 * twos:2].set(giver - passed).at[2:2 + 2 * twos:2].set(receiver + passed)
    return tallies[jax.random.permutation(jax.random.fold_in(own_key, 2), amount)]


def centred(stream_key, dims, deviation, limit, split=(), kind=jnp.bfloat16):
    gain = level_of(stream_key, dims, split, -0.22, 0.18) if split else 1.0
    values = jax.random.normal(stream_key, dims, jnp.float32) * deviation * gain
    return jnp.minimum(jnp.maximum(values, -limit), limit).astype(kind)


def setup_inputs(seed: int = 0) -> dict:
    keys = jax.random.split(jax.random.key(seed), 6)
    queries = draw_queries(jax.random.fold_in(keys[5], 71), 0)
    key_rows = draw_key_rows(jax.random.fold_in(keys[5], 71), 0)
    value_rows = centred(keys[2], (TOKENS, KV * HD), 1.0, 6.0, ((0, 512),))
    out_grad = centred(keys[3], (TOKENS, HQ * HD), 1.0, 6.0, ((0, 512),))
    doc_lengths = ragged(keys[4], NDOC, NBLK, MOST_BLK, 2).astype(jnp.int32)
    return {"queries": queries, "key_rows": key_rows, "value_rows": value_rows, "out_grad": out_grad, "doc_lengths": doc_lengths}


MASK_FILL = -1e+30

def lifted(row_data):
    return lax.optimization_barrier(row_data).astype(jnp.float32)

def doc_index(doc_lengths, first_place, row_count):
    doc_ends = jnp.cumsum(doc_lengths).astype(jnp.int32) * BLK
    places = first_place + jnp.arange(row_count, dtype=jnp.int32)
    labels = lax.optimization_barrier(jnp.sum((places[:, None] >= doc_ends[None, :]).astype(jnp.int32), axis=1))
    return jnp.where(places < 0, -1, labels)

def reference(queries, key_rows, value_rows, out_grad, doc_lengths):
    score_scale = 1.0 / math.sqrt(HD)
    group_size = HQ // KV
    window = MOST_BLK * BLK
    margin = window - BLK
    block_count = TOKENS // BLK
    labels = doc_index(doc_lengths, 0, TOKENS)
    query_all = queries.reshape(TOKENS, KV, group_size, HD)
    grad_all = out_grad.reshape(TOKENS, KV, group_size, HD)
    key_all = key_rows.reshape(TOKENS, KV, HD)
    value_all = value_rows.reshape(TOKENS, KV, HD)
    key_front = jnp.concatenate([jnp.zeros((margin, KV, HD), key_rows.dtype), key_all], axis=0)
    value_front = jnp.concatenate([jnp.zeros((margin, KV, HD), value_rows.dtype), value_all], axis=0)
    label_front = jnp.concatenate([jnp.full((margin,), -1, jnp.int32), labels])

    def forward_block(block_index):
        start_place = (block_index * BLK).astype(jnp.int32)
        q_block = lax.dynamic_slice_in_dim(query_all, start_place, BLK, 0).astype(jnp.float32)
        g_block = lax.dynamic_slice_in_dim(grad_all, start_place, BLK, 0).astype(jnp.float32)
        k_window = lax.dynamic_slice_in_dim(key_front, start_place, window, 0).astype(jnp.float32)
        v_window = lax.dynamic_slice_in_dim(value_front, start_place, window, 0).astype(jnp.float32)
        q_label = lax.dynamic_slice_in_dim(labels, start_place, BLK, 0)
        k_label = lax.dynamic_slice_in_dim(label_front, start_place, window, 0)
        q_place = start_place + jnp.arange(BLK, dtype=jnp.int32)
        k_place = start_place - margin + jnp.arange(window, dtype=jnp.int32)
        allowed = (q_label[:, None] == k_label[None, :]) & (k_place[None, :] <= q_place[:, None])
        scores = jnp.einsum('qkgd,skd->kgqs', q_block, k_window) * score_scale
        scores = jnp.where(allowed, scores, MASK_FILL)
        highest = lax.optimization_barrier(jnp.max(scores, axis=-1, keepdims=True))
        log_total = highest + jnp.log(lax.optimization_barrier(jnp.sum(jnp.exp(scores - highest), axis=-1, keepdims=True)))
        weights = jnp.exp(scores - log_total)
        probs_bf = weights.astype(jnp.bfloat16)
        attn_rows = jnp.einsum('kgqs,skd->qkgd', lifted(probs_bf), v_window).astype(jnp.bfloat16)
        row_delta = jnp.einsum('qkgd,qkgd->kgq', g_block, lifted(attn_rows))
        dprobs = jnp.einsum('qkgd,skd->kgqs', g_block, v_window)
        dscores = (weights * (dprobs - row_delta[..., None])).astype(jnp.bfloat16)
        grad_q = jnp.einsum('kgqs,skd->qkgd', lifted(dscores), k_window) * score_scale
        return (attn_rows, grad_q.astype(jnp.bfloat16), log_total[..., 0], row_delta)
    attn_blocks, dq_blocks, lse_blocks, delta_blocks = lax.map(forward_block, jnp.arange(block_count, dtype=jnp.int32))
    attn_out = attn_blocks.reshape(TOKENS, HQ * HD)
    grad_queries = dq_blocks.reshape(TOKENS, HQ * HD)
    log_all = jnp.transpose(lse_blocks, (0, 3, 1, 2)).reshape(TOKENS, KV, group_size)
    delta_all = jnp.transpose(delta_blocks, (0, 3, 1, 2)).reshape(TOKENS, KV, group_size)
    query_back = jnp.concatenate([query_all, jnp.zeros((margin, KV, group_size, HD), queries.dtype)], axis=0)
    grad_back = jnp.concatenate([grad_all, jnp.zeros((margin, KV, group_size, HD), out_grad.dtype)], axis=0)
    log_back = jnp.concatenate([log_all, jnp.zeros((margin, KV, group_size), jnp.float32)], axis=0)
    delta_back = jnp.concatenate([delta_all, jnp.zeros((margin, KV, group_size), jnp.float32)], axis=0)
    label_back = jnp.concatenate([labels, jnp.full((margin,), -2, jnp.int32)])

    def key_block(block_index):
        start_place = (block_index * BLK).astype(jnp.int32)
        k_block = lax.dynamic_slice_in_dim(key_all, start_place, BLK, 0).astype(jnp.float32)
        v_block = lax.dynamic_slice_in_dim(value_all, start_place, BLK, 0).astype(jnp.float32)
        q_window = lax.dynamic_slice_in_dim(query_back, start_place, window, 0).astype(jnp.float32)
        g_window = lax.dynamic_slice_in_dim(grad_back, start_place, window, 0).astype(jnp.float32)
        log_window = jnp.transpose(lax.dynamic_slice_in_dim(log_back, start_place, window, 0), (1, 2, 0))
        delta_window = jnp.transpose(lax.dynamic_slice_in_dim(delta_back, start_place, window, 0), (1, 2, 0))
        q_label = lax.dynamic_slice_in_dim(label_back, start_place, window, 0)
        k_label = lax.dynamic_slice_in_dim(labels, start_place, BLK, 0)
        q_place = start_place + jnp.arange(window, dtype=jnp.int32)
        k_place = start_place + jnp.arange(BLK, dtype=jnp.int32)
        allowed = (q_label[:, None] == k_label[None, :]) & (k_place[None, :] <= q_place[:, None])
        scores = jnp.einsum('qkgd,skd->kgqs', q_window, k_block) * score_scale
        weights = jnp.exp(jnp.where(allowed, scores - log_window[..., None], MASK_FILL))
        probs_bf = weights.astype(jnp.bfloat16)
        dprobs = jnp.einsum('qkgd,skd->kgqs', g_window, v_block)
        dscores = (weights * (dprobs - delta_window[..., None])).astype(jnp.bfloat16)
        grad_k = jnp.einsum('kgqs,qkgd->skd', lifted(dscores), q_window) * score_scale
        grad_v = jnp.einsum('kgqs,qkgd->skd', lifted(probs_bf), g_window)
        return (grad_k.astype(jnp.bfloat16), grad_v.astype(jnp.bfloat16))
    dk_blocks, dv_blocks = lax.map(key_block, jnp.arange(block_count, dtype=jnp.int32))
    grad_keys = dk_blocks.reshape(TOKENS, KV * HD)
    grad_values = dv_blocks.reshape(TOKENS, KV * HD)
    return (attn_out, grad_queries, grad_keys, grad_values)
```

```python
import math

import jax
import jax.numpy as jnp
from jax import lax
from jax.sharding import PartitionSpec as P

HD = 128
BLK = 128
MOST_BLK = 16
Q_ROWS = 256


MASK_FILL = -1e30


def passed_along(value, axis, steps):
    count = lax.axis_size(axis)
    first, last = (max(0, -steps), min(count, count - steps))
    return lax.ppermute(value, axis, [(source, source + steps) for source in range(first, last)])


def lifted(row_data):
    return lax.optimization_barrier(row_data).astype(jnp.float32)


def doc_index(doc_lengths, first_place, row_count):
    doc_ends = jnp.cumsum(doc_lengths) * BLK
    places = first_place + jnp.arange(row_count, dtype=jnp.int32)
    labels = jnp.sum((places[:, None] >= doc_ends[None, :]).astype(jnp.int32), axis=1)
    return jnp.where(places < 0, -1, labels)


def widen_heads(row_data, copies):
    tokens_here = row_data.shape[0]
    head_count = row_data.shape[1] // HD
    shaped = row_data.reshape(tokens_here, head_count, 1, HD)
    shaped = jnp.broadcast_to(shaped, (tokens_here, head_count, copies, HD))
    return shaped.reshape(tokens_here, head_count * copies * HD)


def block_pass(q_block, g_block, k_win, v_win, allowed, score_scale):
    scores = (
        jnp.einsum("qhd,kd->hqk", q_block, k_win, preferred_element_type=jnp.float32)
        * score_scale
    )
    scores = jnp.where(allowed[None], scores, MASK_FILL)
    highest = jnp.max(scores, axis=-1, keepdims=True)
    row_total = jnp.sum(jnp.exp(scores - highest), axis=-1, keepdims=True)
    log_total = highest + jnp.log(row_total)
    weights = jnp.exp(scores - log_total)
    probs_bf = weights.astype(jnp.bfloat16)
    attn_block = jnp.einsum(
        "hqk,kd->qhd", probs_bf, v_win, preferred_element_type=jnp.float32
    ).astype(jnp.bfloat16)
    row_delta = jnp.transpose(jnp.sum(lifted(g_block) * lifted(attn_block), axis=-1), (1, 0))
    dprobs = jnp.einsum("qhd,kd->hqk", g_block, v_win, preferred_element_type=jnp.float32)
    dscores = (weights * (dprobs - row_delta[..., None])).astype(jnp.bfloat16)
    dq_block = (
        jnp.einsum("hqk,kd->qhd", dscores, k_win, preferred_element_type=jnp.float32)
        * score_scale
    ).astype(jnp.bfloat16)
    grad_k = jnp.einsum("hqk,qhd->kd", dscores, q_block, preferred_element_type=jnp.float32)
    grad_v = jnp.einsum("hqk,qhd->kd", probs_bf, g_block, preferred_element_type=jnp.float32)
    return attn_block, dq_block, grad_k, grad_v


def local(queries, key_rows, value_rows, out_grad, doc_lengths):
    seq_width = lax.axis_size("sp")
    tok_dev = queries.shape[0]
    span_rows = tok_dev * seq_width
    heads_q = queries.shape[1] // HD
    heads_k = key_rows.shape[1] // HD
    local_q = heads_q // seq_width
    copies = seq_width // heads_k
    score_scale = 1.0 / math.sqrt(HD)
    q_seq, g_seq = (
        lax.all_to_all(queries, "sp", split_axis=1, concat_axis=0, tiled=True),
        lax.all_to_all(out_grad, "sp", split_axis=1, concat_axis=0, tiled=True),
    )
    k_seq, v_seq = (
        lax.all_to_all(
            widen_heads(key_rows, copies), "sp", split_axis=1, concat_axis=0, tiled=True
        ),
        lax.all_to_all(
            widen_heads(value_rows, copies), "sp", split_axis=1, concat_axis=0, tiled=True
        ),
    )
    reach = MOST_BLK * BLK
    reach_groups = (reach - 1) // span_rows + 1
    first_place = lax.axis_index("fsdp") * span_rows
    earlier = [passed_along((k_seq, v_seq), "fsdp", d) for d in range(reach_groups, 0, -1)]
    k_all = jnp.concatenate([piece[0] for piece in earlier] + [k_seq], axis=0)
    v_all = jnp.concatenate([piece[1] for piece in earlier] + [v_seq], axis=0)
    base_place = first_place - reach_groups * span_rows
    key_count = (reach_groups + 1) * span_rows
    labels = doc_index(doc_lengths, base_place, key_count)
    places = base_place + jnp.arange(key_count, dtype=jnp.int32)
    window = reach + Q_ROWS
    own_start = reach_groups * span_rows
    grad_k_all = jnp.zeros((key_count, HD), jnp.float32)
    grad_v_all = jnp.zeros((key_count, HD), jnp.float32)
    attn_parts, dq_parts = [], []
    for block in range(span_rows // Q_ROWS):
        q_lo = block * Q_ROWS
        k_lo = own_start + q_lo + Q_ROWS - window
        q_label = labels[own_start + q_lo : own_start + q_lo + Q_ROWS]
        q_place = places[own_start + q_lo : own_start + q_lo + Q_ROWS]
        k_label = labels[k_lo : k_lo + window]
        k_place = places[k_lo : k_lo + window]
        allowed = (q_label[:, None] == k_label[None, :]) & (k_place[None, :] <= q_place[:, None])
        q_block = q_seq[q_lo : q_lo + Q_ROWS].reshape(Q_ROWS, local_q, HD)
        g_block = g_seq[q_lo : q_lo + Q_ROWS].reshape(Q_ROWS, local_q, HD)
        attn_block, dq_block, grad_k, grad_v = block_pass(
            q_block,
            g_block,
            k_all[k_lo : k_lo + window],
            v_all[k_lo : k_lo + window],
            allowed,
            score_scale,
        )
        attn_parts.append(attn_block.reshape(Q_ROWS, local_q * HD))
        dq_parts.append(dq_block.reshape(Q_ROWS, local_q * HD))
        grad_k_all = grad_k_all.at[k_lo : k_lo + window].add(grad_k)
        grad_v_all = grad_v_all.at[k_lo : k_lo + window].add(grad_v)
    key_sum = grad_k_all[own_start:]
    value_sum = grad_v_all[own_start:]
    for distance in range(1, reach_groups + 1):
        lo = (reach_groups - distance) * span_rows
        back_k, back_v = passed_along(
            (
                grad_k_all[lo : lo + span_rows].astype(jnp.bfloat16),
                grad_v_all[lo : lo + span_rows].astype(jnp.bfloat16),
            ),
            "fsdp",
            -distance,
        )
        key_sum = key_sum + back_k
        value_sum = value_sum + back_v
    key_back, value_back = (
        lax.all_to_all(
            (key_sum * score_scale).astype(jnp.bfloat16),
            "sp",
            split_axis=0,
            concat_axis=1,
            tiled=True,
        ),
        lax.all_to_all(
            value_sum.astype(jnp.bfloat16), "sp", split_axis=0, concat_axis=1, tiled=True
        ),
    )
    grad_keys = jnp.sum(
        key_back.astype(jnp.float32).reshape(tok_dev, heads_k, copies, HD), axis=2
    ).reshape(tok_dev, heads_k * HD)
    grad_values = jnp.sum(
        value_back.astype(jnp.float32).reshape(tok_dev, heads_k, copies, HD), axis=2
    ).reshape(tok_dev, heads_k * HD)
    attn_seq = jnp.concatenate(attn_parts, axis=0)
    dq_seq = jnp.concatenate(dq_parts, axis=0)
    attn_out, grad_queries = (
        lax.all_to_all(attn_seq, "sp", split_axis=0, concat_axis=1, tiled=True),
        lax.all_to_all(dq_seq, "sp", split_axis=0, concat_axis=1, tiled=True),
    )
    return (
        attn_out,
        grad_queries,
        grad_keys.astype(jnp.bfloat16),
        grad_values.astype(jnp.bfloat16),
    )


def solution(mesh):
    in_specs = (
        P(("fsdp", "sp"), None),
        P(("fsdp", "sp"), None),
        P(("fsdp", "sp"), None),
        P(("fsdp", "sp"), None),
        P(),
    )
    out_specs = (
        P(("fsdp", "sp"), None),
        P(("fsdp", "sp"), None),
        P(("fsdp", "sp"), None),
        P(("fsdp", "sp"), None),
    )
    return jax.shard_map(local, mesh=mesh, in_specs=in_specs, out_specs=out_specs, check_vma=False)
```

```python
import math

import jax
import jax.numpy as jnp
from jax import lax
from jax.sharding import PartitionSpec as P

HD = 128
BLK = 128
MOST_BLK = 16
Q_ROWS = 256


MASK_FILL = -1e30


def passed_along(value, axis, steps):
    count = lax.axis_size(axis)
    first, last = (max(0, -steps), min(count, count - steps))
    return lax.ppermute(value, axis, [(source, source + steps) for source in range(first, last)])


def lifted(row_data):
    return lax.optimization_barrier(row_data).astype(jnp.float32)


def doc_index(doc_lengths, first_place, row_count):
    doc_ends = jnp.cumsum(doc_lengths) * BLK
    places = first_place + jnp.arange(row_count, dtype=jnp.int32)
    labels = jnp.sum((places[:, None] >= doc_ends[None, :]).astype(jnp.int32), axis=1)
    return jnp.where(places < 0, -1, labels)


def widen_heads(row_data, copies):
    tokens_here = row_data.shape[0]
    head_count = row_data.shape[1] // HD
    shaped = row_data.reshape(tokens_here, head_count, 1, HD)
    shaped = jnp.broadcast_to(shaped, (tokens_here, head_count, copies, HD))
    return shaped.reshape(tokens_here, head_count * copies * HD)


def block_pass(q_block, g_block, k_win, v_win, allowed, score_scale):
    scores = (
        jnp.einsum("qhd,kd->hqk", q_block, k_win, preferred_element_type=jnp.float32)
        * score_scale
    )
    scores = jnp.where(allowed[None], scores, MASK_FILL)
    highest = jnp.max(scores, axis=-1, keepdims=True)
    row_total = jnp.sum(jnp.exp(scores - highest), axis=-1, keepdims=True)
    log_total = highest + jnp.log(row_total)
    weights = jnp.exp(scores - log_total)
    probs_bf = weights.astype(jnp.bfloat16)
    attn_block = jnp.einsum(
        "hqk,kd->qhd", probs_bf, v_win, preferred_element_type=jnp.float32
    ).astype(jnp.bfloat16)
    row_delta = jnp.transpose(jnp.sum(lifted(g_block) * lifted(attn_block), axis=-1), (1, 0))
    dprobs = jnp.einsum("qhd,kd->hqk", g_block, v_win, preferred_element_type=jnp.float32)
    dscores = (weights * (dprobs - row_delta[..., None])).astype(jnp.bfloat16)
    dq_block = (
        jnp.einsum("hqk,kd->qhd", dscores, k_win, preferred_element_type=jnp.float32)
        * score_scale
    ).astype(jnp.bfloat16)
    grad_k = jnp.einsum("hqk,qhd->kd", dscores, q_block, preferred_element_type=jnp.float32)
    grad_v = jnp.einsum("hqk,qhd->kd", probs_bf, g_block, preferred_element_type=jnp.float32)
    return attn_block, dq_block, grad_k, grad_v


def local(queries, key_rows, value_rows, out_grad, doc_lengths):
    seq_width = lax.axis_size("sp")
    tok_dev = queries.shape[0]
    span_rows = tok_dev * seq_width
    heads_q = queries.shape[1] // HD
    heads_k = key_rows.shape[1] // HD
    local_q = heads_q // seq_width
    copies = seq_width // heads_k
    score_scale = 1.0 / math.sqrt(HD)
    packed = jnp.concatenate(
        [
            queries.reshape(tok_dev, seq_width, local_q * HD),
            out_grad.reshape(tok_dev, seq_width, local_q * HD),
            widen_heads(key_rows, copies).reshape(tok_dev, seq_width, HD),
            widen_heads(value_rows, copies).reshape(tok_dev, seq_width, HD),
        ],
        axis=2,
    )
    packed = lax.all_to_all(packed, "sp", split_axis=1, concat_axis=0, tiled=True)
    packed = packed.reshape(span_rows, packed.shape[-1])
    q_width = local_q * HD
    q_seq = packed[:, :q_width]
    g_seq = packed[:, q_width : 2 * q_width]
    kv_seq = packed[:, 2 * q_width :]
    reach = MOST_BLK * BLK
    reach_groups = (reach - 1) // span_rows + 1
    first_place = lax.axis_index("fsdp") * span_rows
    earlier = [passed_along(kv_seq, "fsdp", d) for d in range(reach_groups, 0, -1)]
    kv_all = jnp.concatenate(earlier + [kv_seq], axis=0)
    k_all = kv_all[:, :HD]
    v_all = kv_all[:, HD:]
    base_place = first_place - reach_groups * span_rows
    key_count = (reach_groups + 1) * span_rows
    labels = doc_index(doc_lengths, base_place, key_count)
    places = base_place + jnp.arange(key_count, dtype=jnp.int32)
    window = reach + Q_ROWS
    own_start = reach_groups * span_rows
    grad_k_all = jnp.zeros((key_count, HD), jnp.float32)
    grad_v_all = jnp.zeros((key_count, HD), jnp.float32)
    attn_parts, dq_parts = [], []
    for block in range(span_rows // Q_ROWS):
        q_lo = block * Q_ROWS
        k_lo = own_start + q_lo + Q_ROWS - window
        q_label = labels[own_start + q_lo : own_start + q_lo + Q_ROWS]
        q_place = places[own_start + q_lo : own_start + q_lo + Q_ROWS]
        k_label = labels[k_lo : k_lo + window]
        k_place = places[k_lo : k_lo + window]
        allowed = (q_label[:, None] == k_label[None, :]) & (k_place[None, :] <= q_place[:, None])
        q_block = q_seq[q_lo : q_lo + Q_ROWS].reshape(Q_ROWS, local_q, HD)
        g_block = g_seq[q_lo : q_lo + Q_ROWS].reshape(Q_ROWS, local_q, HD)
        attn_block, dq_block, grad_k, grad_v = block_pass(
            q_block,
            g_block,
            k_all[k_lo : k_lo + window],
            v_all[k_lo : k_lo + window],
            allowed,
            score_scale,
        )
        attn_parts.append(attn_block.reshape(Q_ROWS, local_q * HD))
        dq_parts.append(dq_block.reshape(Q_ROWS, local_q * HD))
        grad_k_all = grad_k_all.at[k_lo : k_lo + window].add(grad_k)
        grad_v_all = grad_v_all.at[k_lo : k_lo + window].add(grad_v)
    grad_kv_all = jnp.concatenate([grad_k_all, grad_v_all], axis=1)
    kv_sum = grad_kv_all[own_start:]
    for distance in range(1, reach_groups + 1):
        lo = (reach_groups - distance) * span_rows
        back = passed_along(
            grad_kv_all[lo : lo + span_rows].astype(jnp.bfloat16), "fsdp", -distance
        )
        kv_sum = kv_sum + back
    kv_sum = jnp.concatenate([kv_sum[:, :HD] * score_scale, kv_sum[:, HD:]], axis=1)
    attn_seq = jnp.concatenate(attn_parts, axis=0)
    dq_seq = jnp.concatenate(dq_parts, axis=0)
    outgoing = jnp.concatenate([attn_seq, dq_seq, kv_sum.astype(jnp.bfloat16)], axis=1)
    back_all = lax.all_to_all(outgoing, "sp", split_axis=0, concat_axis=1, tiled=True)
    back_all = back_all.reshape(tok_dev, seq_width, outgoing.shape[1])
    attn_out = back_all[:, :, :q_width].reshape(tok_dev, heads_q * HD)
    grad_queries = back_all[:, :, q_width : 2 * q_width].reshape(tok_dev, heads_q * HD)
    kv_back = back_all[:, :, 2 * q_width :].astype(jnp.float32)
    grad_keys = jnp.sum(
        kv_back[:, :, :HD].reshape(tok_dev, heads_k, copies, HD), axis=2
    ).reshape(tok_dev, heads_k * HD)
    grad_values = jnp.sum(
        kv_back[:, :, HD:].reshape(tok_dev, heads_k, copies, HD), axis=2
    ).reshape(tok_dev, heads_k * HD)
    return (
        attn_out,
        grad_queries,
        grad_keys.astype(jnp.bfloat16),
        grad_values.astype(jnp.bfloat16),
    )


def solution(mesh):
    in_specs = (
        P(("fsdp", "sp"), None),
        P(("fsdp", "sp"), None),
        P(("fsdp", "sp"), None),
        P(("fsdp", "sp"), None),
        P(),
    )
    out_specs = (
        P(("fsdp", "sp"), None),
        P(("fsdp", "sp"), None),
        P(("fsdp", "sp"), None),
        P(("fsdp", "sp"), None),
    )
    return jax.shard_map(local, mesh=mesh, in_specs=in_specs, out_specs=out_specs, check_vma=False)
```

```python
import math

import jax
import jax.numpy as jnp
from jax import lax
from jax.sharding import PartitionSpec as P

HD = 128
BLK = 128
MOST_BLK = 16
Q_ROWS = 256


MASK_FILL = -1e30


def passed_along(value, axis, steps):
    count = lax.axis_size(axis)
    first, last = (max(0, -steps), min(count, count - steps))
    return lax.ppermute(value, axis, [(source, source + steps) for source in range(first, last)])


def lifted(row_data):
    return lax.optimization_barrier(row_data).astype(jnp.float32)


def doc_index(doc_lengths, first_place, row_count):
    doc_ends = jnp.cumsum(doc_lengths) * BLK
    places = first_place + jnp.arange(row_count, dtype=jnp.int32)
    labels = jnp.sum((places[:, None] >= doc_ends[None, :]).astype(jnp.int32), axis=1)
    return jnp.where(places < 0, -1, labels)


def widen_heads(row_data, copies):
    tokens_here = row_data.shape[0]
    head_count = row_data.shape[1] // HD
    shaped = row_data.reshape(tokens_here, head_count, 1, HD)
    shaped = jnp.broadcast_to(shaped, (tokens_here, head_count, copies, HD))
    return shaped.reshape(tokens_here, head_count * copies * HD)


def block_pass(q_block, g_block, k_win, v_win, allowed, score_scale):
    scores = (
        jnp.einsum("qhd,kd->hqk", q_block, k_win, preferred_element_type=jnp.float32)
        * score_scale
    )
    scores = jnp.where(allowed[None], scores, MASK_FILL)
    highest = jnp.max(scores, axis=-1, keepdims=True)
    row_total = jnp.sum(jnp.exp(scores - highest), axis=-1, keepdims=True)
    log_total = highest + jnp.log(row_total)
    weights = jnp.exp(scores - log_total)
    probs_bf = weights.astype(jnp.bfloat16)
    attn_block = jnp.einsum(
        "hqk,kd->qhd", probs_bf, v_win, preferred_element_type=jnp.float32
    ).astype(jnp.bfloat16)
    row_delta = jnp.transpose(jnp.sum(lifted(g_block) * lifted(attn_block), axis=-1), (1, 0))
    dprobs = jnp.einsum("qhd,kd->hqk", g_block, v_win, preferred_element_type=jnp.float32)
    dscores = (weights * (dprobs - row_delta[..., None])).astype(jnp.bfloat16)
    dq_block = (
        jnp.einsum("hqk,kd->qhd", dscores, k_win, preferred_element_type=jnp.float32)
        * score_scale
    ).astype(jnp.bfloat16)
    grad_k = jnp.einsum("hqk,qhd->kd", dscores, q_block, preferred_element_type=jnp.float32)
    grad_v = jnp.einsum("hqk,qhd->kd", probs_bf, g_block, preferred_element_type=jnp.float32)
    return attn_block, dq_block, grad_k, grad_v


def local(queries, key_rows, value_rows, out_grad, doc_lengths):
    seq_width = lax.axis_size("sp")
    tok_dev = queries.shape[0]
    span_rows = tok_dev * seq_width
    heads_q = queries.shape[1] // HD
    heads_k = key_rows.shape[1] // HD
    local_q = heads_q // seq_width
    copies = seq_width // heads_k
    score_scale = 1.0 / math.sqrt(HD)
    kv_pack = jnp.concatenate(
        [
            widen_heads(key_rows, copies).reshape(tok_dev, seq_width, HD),
            widen_heads(value_rows, copies).reshape(tok_dev, seq_width, HD),
        ],
        axis=2,
    )
    kv_seq = lax.all_to_all(kv_pack, "sp", split_axis=1, concat_axis=0, tiled=True)
    kv_seq = kv_seq.reshape(span_rows, 2 * HD)
    q_width = local_q * HD
    qg_pack = jnp.concatenate(
        [
            queries.reshape(tok_dev, seq_width, q_width),
            out_grad.reshape(tok_dev, seq_width, q_width),
        ],
        axis=2,
    )
    qg_seq = lax.all_to_all(qg_pack, "sp", split_axis=1, concat_axis=0, tiled=True)
    qg_seq = qg_seq.reshape(span_rows, 2 * q_width)
    q_seq = qg_seq[:, :q_width]
    g_seq = qg_seq[:, q_width:]
    reach = MOST_BLK * BLK
    reach_groups = (reach - 1) // span_rows + 1
    first_place = lax.axis_index("fsdp") * span_rows
    earlier = [passed_along(kv_seq, "fsdp", d) for d in range(reach_groups, 0, -1)]
    kv_all = jnp.concatenate(earlier + [kv_seq], axis=0)
    k_all = kv_all[:, :HD]
    v_all = kv_all[:, HD:]
    base_place = first_place - reach_groups * span_rows
    key_count = (reach_groups + 1) * span_rows
    labels = doc_index(doc_lengths, base_place, key_count)
    places = base_place + jnp.arange(key_count, dtype=jnp.int32)
    window = reach + Q_ROWS
    own_start = reach_groups * span_rows
    grad_k_all = jnp.zeros((key_count, HD), jnp.float32)
    grad_v_all = jnp.zeros((key_count, HD), jnp.float32)
    attn_parts, dq_parts = [], []
    for block in range(span_rows // Q_ROWS):
        q_lo = block * Q_ROWS
        k_lo = own_start + q_lo + Q_ROWS - window
        q_label = labels[own_start + q_lo : own_start + q_lo + Q_ROWS]
        q_place = places[own_start + q_lo : own_start + q_lo + Q_ROWS]
        k_label = labels[k_lo : k_lo + window]
        k_place = places[k_lo : k_lo + window]
        allowed = (q_label[:, None] == k_label[None, :]) & (k_place[None, :] <= q_place[:, None])
        q_block = q_seq[q_lo : q_lo + Q_ROWS].reshape(Q_ROWS, local_q, HD)
        g_block = g_seq[q_lo : q_lo + Q_ROWS].reshape(Q_ROWS, local_q, HD)
        attn_block, dq_block, grad_k, grad_v = block_pass(
            q_block,
            g_block,
            k_all[k_lo : k_lo + window],
            v_all[k_lo : k_lo + window],
            allowed,
            score_scale,
        )
        attn_parts.append(attn_block.reshape(Q_ROWS, local_q * HD))
        dq_parts.append(dq_block.reshape(Q_ROWS, local_q * HD))
        grad_k_all = grad_k_all.at[k_lo : k_lo + window].add(grad_k)
        grad_v_all = grad_v_all.at[k_lo : k_lo + window].add(grad_v)
    grad_kv_all = jnp.concatenate([grad_k_all, grad_v_all], axis=1)
    backs = [
        passed_along(
            grad_kv_all[lo : lo + span_rows].astype(jnp.bfloat16), "fsdp", -distance
        )
        for distance, lo in (
            (d, (reach_groups - d) * span_rows) for d in range(1, reach_groups + 1)
        )
    ]
    attn_seq = jnp.concatenate(attn_parts, axis=0)
    dq_seq = jnp.concatenate(dq_parts, axis=0)
    outgoing = jnp.concatenate([attn_seq, dq_seq], axis=1)
    back_all = lax.all_to_all(outgoing, "sp", split_axis=0, concat_axis=1, tiled=True)
    back_all = back_all.reshape(tok_dev, seq_width, outgoing.shape[1])
    attn_out = back_all[:, :, :q_width].reshape(tok_dev, heads_q * HD)
    grad_queries = back_all[:, :, q_width:].reshape(tok_dev, heads_q * HD)
    kv_sum = grad_kv_all[own_start:]
    for back in backs:
        kv_sum = kv_sum + back
    kv_sum = jnp.concatenate([kv_sum[:, :HD] * score_scale, kv_sum[:, HD:]], axis=1)
    kv_back = lax.all_to_all(
        kv_sum.astype(jnp.bfloat16), "sp", split_axis=0, concat_axis=1, tiled=True
    )
    kv_back = kv_back.reshape(tok_dev, seq_width, 2 * HD).astype(jnp.float32)
    grad_keys = jnp.sum(
        kv_back[:, :, :HD].reshape(tok_dev, heads_k, copies, HD), axis=2
    ).reshape(tok_dev, heads_k * HD)
    grad_values = jnp.sum(
        kv_back[:, :, HD:].reshape(tok_dev, heads_k, copies, HD), axis=2
    ).reshape(tok_dev, heads_k * HD)
    return (
        attn_out,
        grad_queries,
        grad_keys.astype(jnp.bfloat16),
        grad_values.astype(jnp.bfloat16),
    )


def solution(mesh):
    in_specs = (
        P(("fsdp", "sp"), None),
        P(("fsdp", "sp"), None),
        P(("fsdp", "sp"), None),
        P(("fsdp", "sp"), None),
        P(),
    )
    out_specs = (
        P(("fsdp", "sp"), None),
        P(("fsdp", "sp"), None),
        P(("fsdp", "sp"), None),
        P(("fsdp", "sp"), None),
    )
    return jax.shard_map(local, mesh=mesh, in_specs=in_specs, out_specs=out_specs, check_vma=False)
```

```python
import math

import jax
import jax.numpy as jnp
from jax import lax
from jax.sharding import PartitionSpec as P

HD = 128
BLK = 128
MOST_BLK = 16
Q_ROWS = 256


MASK_FILL = -1e30


def passed_along(value, axis, steps):
    count = lax.axis_size(axis)
    first, last = (max(0, -steps), min(count, count - steps))
    return lax.ppermute(value, axis, [(source, source + steps) for source in range(first, last)])


def lifted(row_data):
    return lax.optimization_barrier(row_data).astype(jnp.float32)


def doc_index(doc_lengths, first_place, row_count):
    doc_ends = jnp.cumsum(doc_lengths) * BLK
    places = first_place + jnp.arange(row_count, dtype=jnp.int32)
    labels = jnp.sum((places[:, None] >= doc_ends[None, :]).astype(jnp.int32), axis=1)
    return jnp.where(places < 0, -1, labels)


def widen_heads(row_data, copies):
    tokens_here = row_data.shape[0]
    head_count = row_data.shape[1] // HD
    shaped = row_data.reshape(tokens_here, head_count, 1, HD)
    shaped = jnp.broadcast_to(shaped, (tokens_here, head_count, copies, HD))
    return shaped.reshape(tokens_here, head_count * copies * HD)


def block_pass(q_block, g_block, k_win, v_win, allowed, score_scale):
    scores = (
        jnp.einsum("qhd,kd->hqk", q_block, k_win, preferred_element_type=jnp.float32)
        * score_scale
    )
    scores = jnp.where(allowed[None], scores, MASK_FILL)
    highest = jnp.max(scores, axis=-1, keepdims=True)
    row_total = jnp.sum(jnp.exp(scores - highest), axis=-1, keepdims=True)
    log_total = highest + jnp.log(row_total)
    weights = jnp.exp(scores - log_total)
    probs_bf = weights.astype(jnp.bfloat16)
    attn_block = jnp.einsum(
        "hqk,kd->qhd", probs_bf, v_win, preferred_element_type=jnp.float32
    ).astype(jnp.bfloat16)
    row_delta = jnp.transpose(jnp.sum(lifted(g_block) * lifted(attn_block), axis=-1), (1, 0))
    dprobs = jnp.einsum("qhd,kd->hqk", g_block, v_win, preferred_element_type=jnp.float32)
    dscores = (weights * (dprobs - row_delta[..., None])).astype(jnp.bfloat16)
    dq_block = (
        jnp.einsum("hqk,kd->qhd", dscores, k_win, preferred_element_type=jnp.float32)
        * score_scale
    ).astype(jnp.bfloat16)
    grad_k = jnp.einsum("hqk,qhd->kd", dscores, q_block, preferred_element_type=jnp.float32)
    grad_v = jnp.einsum("hqk,qhd->kd", probs_bf, g_block, preferred_element_type=jnp.float32)
    return attn_block, dq_block, grad_k, grad_v


def local(queries, key_rows, value_rows, out_grad, doc_lengths):
    seq_width = lax.axis_size("sp")
    tok_dev = queries.shape[0]
    span_rows = tok_dev * seq_width
    heads_q = queries.shape[1] // HD
    heads_k = key_rows.shape[1] // HD
    local_q = heads_q // seq_width
    copies = seq_width // heads_k
    score_scale = 1.0 / math.sqrt(HD)
    kv_pack = jnp.concatenate(
        [
            widen_heads(key_rows, copies).reshape(tok_dev, seq_width, HD),
            widen_heads(value_rows, copies).reshape(tok_dev, seq_width, HD),
        ],
        axis=2,
    )
    kv_seq = lax.all_to_all(kv_pack, "sp", split_axis=1, concat_axis=0, tiled=True)
    kv_seq = kv_seq.reshape(span_rows, 2 * HD)
    q_width = local_q * HD
    qg_pack = jnp.concatenate(
        [
            queries.reshape(tok_dev, seq_width, q_width),
            out_grad.reshape(tok_dev, seq_width, q_width),
        ],
        axis=2,
    )
    qg_seq = lax.all_to_all(qg_pack, "sp", split_axis=1, concat_axis=0, tiled=True)
    qg_seq = qg_seq.reshape(span_rows, 2 * q_width)
    q_seq = qg_seq[:, :q_width]
    g_seq = qg_seq[:, q_width:]
    reach = MOST_BLK * BLK
    reach_groups = (reach - 1) // span_rows + 1
    first_place = lax.axis_index("fsdp") * span_rows
    core = lax.axis_index("sp") % 2
    half = span_rows // 2
    sibling = [(s, s ^ 1) for s in range(seq_width)]
    my_half = lax.dynamic_slice_in_dim(kv_seq, core * half, half, 0)
    received = [passed_along(my_half, "fsdp", d) for d in range(reach_groups, 0, -1)]
    swapped = lax.ppermute(jnp.concatenate(received, axis=0), "sp", sibling)
    earlier = []
    for index, mine in enumerate(received):
        theirs = swapped[index * half : (index + 1) * half]
        earlier.append(
            jnp.where(
                core == 0,
                jnp.concatenate([mine, theirs], axis=0),
                jnp.concatenate([theirs, mine], axis=0),
            )
        )
    kv_all = jnp.concatenate(earlier + [kv_seq], axis=0)
    k_all = kv_all[:, :HD]
    v_all = kv_all[:, HD:]
    base_place = first_place - reach_groups * span_rows
    key_count = (reach_groups + 1) * span_rows
    labels = doc_index(doc_lengths, base_place, key_count)
    places = base_place + jnp.arange(key_count, dtype=jnp.int32)
    window = reach + Q_ROWS
    own_start = reach_groups * span_rows
    grad_k_all = jnp.zeros((key_count, HD), jnp.float32)
    grad_v_all = jnp.zeros((key_count, HD), jnp.float32)
    attn_parts, dq_parts = [], []
    for block in range(span_rows // Q_ROWS):
        q_lo = block * Q_ROWS
        k_lo = own_start + q_lo + Q_ROWS - window
        q_label = labels[own_start + q_lo : own_start + q_lo + Q_ROWS]
        q_place = places[own_start + q_lo : own_start + q_lo + Q_ROWS]
        k_label = labels[k_lo : k_lo + window]
        k_place = places[k_lo : k_lo + window]
        allowed = (q_label[:, None] == k_label[None, :]) & (k_place[None, :] <= q_place[:, None])
        q_block = q_seq[q_lo : q_lo + Q_ROWS].reshape(Q_ROWS, local_q, HD)
        g_block = g_seq[q_lo : q_lo + Q_ROWS].reshape(Q_ROWS, local_q, HD)
        attn_block, dq_block, grad_k, grad_v = block_pass(
            q_block,
            g_block,
            k_all[k_lo : k_lo + window],
            v_all[k_lo : k_lo + window],
            allowed,
            score_scale,
        )
        attn_parts.append(attn_block.reshape(Q_ROWS, local_q * HD))
        dq_parts.append(dq_block.reshape(Q_ROWS, local_q * HD))
        grad_k_all = grad_k_all.at[k_lo : k_lo + window].add(grad_k)
        grad_v_all = grad_v_all.at[k_lo : k_lo + window].add(grad_v)
    grad_kv_all = jnp.concatenate([grad_k_all, grad_v_all], axis=1)
    earlier_parts = grad_kv_all[:own_start].reshape(reach_groups, 2, half, 2 * HD)
    mine_part = lax.dynamic_index_in_dim(earlier_parts, core, 1, keepdims=False)
    their_part = lax.dynamic_index_in_dim(earlier_parts, 1 - core, 1, keepdims=False)
    pair_sum = mine_part + lax.ppermute(their_part, "sp", sibling)
    backs = [
        passed_along(pair_sum[reach_groups - d].astype(jnp.bfloat16), "fsdp", -d)
        for d in range(1, reach_groups + 1)
    ]
    attn_seq = jnp.concatenate(attn_parts, axis=0)
    dq_seq = jnp.concatenate(dq_parts, axis=0)
    outgoing = jnp.concatenate([attn_seq, dq_seq], axis=1)
    back_all = lax.all_to_all(outgoing, "sp", split_axis=0, concat_axis=1, tiled=True)
    back_all = back_all.reshape(tok_dev, seq_width, outgoing.shape[1])
    attn_out = back_all[:, :, :q_width].reshape(tok_dev, heads_q * HD)
    grad_queries = back_all[:, :, q_width:].reshape(tok_dev, heads_q * HD)
    back_half = backs[0].astype(jnp.float32)
    for back in backs[1:]:
        back_half = back_half + back
    kv_sum = grad_kv_all[own_start:]
    kv_sum = lax.dynamic_update_slice_in_dim(
        kv_sum, lax.dynamic_slice_in_dim(kv_sum, core * half, half, 0) + back_half, core * half, 0
    )
    kv_sum = jnp.concatenate([kv_sum[:, :HD] * score_scale, kv_sum[:, HD:]], axis=1)
    kv_back = lax.all_to_all(
        kv_sum.astype(jnp.bfloat16), "sp", split_axis=0, concat_axis=1, tiled=True
    )
    kv_back = kv_back.reshape(tok_dev, seq_width, 2 * HD).astype(jnp.float32)
    grad_keys = jnp.sum(
        kv_back[:, :, :HD].reshape(tok_dev, heads_k, copies, HD), axis=2
    ).reshape(tok_dev, heads_k * HD)
    grad_values = jnp.sum(
        kv_back[:, :, HD:].reshape(tok_dev, heads_k, copies, HD), axis=2
    ).reshape(tok_dev, heads_k * HD)
    return (
        attn_out,
        grad_queries,
        grad_keys.astype(jnp.bfloat16),
        grad_values.astype(jnp.bfloat16),
    )


def solution(mesh):
    in_specs = (
        P(("fsdp", "sp"), None),
        P(("fsdp", "sp"), None),
        P(("fsdp", "sp"), None),
        P(("fsdp", "sp"), None),
        P(),
    )
    out_specs = (
        P(("fsdp", "sp"), None),
        P(("fsdp", "sp"), None),
        P(("fsdp", "sp"), None),
        P(("fsdp", "sp"), None),
    )
    return jax.shard_map(local, mesh=mesh, in_specs=in_specs, out_specs=out_specs, check_vma=False)
```

```python
import math

import jax
import jax.numpy as jnp
from jax import lax
from jax.sharding import PartitionSpec as P

HD = 128
BLK = 128
MOST_BLK = 16
Q_ROWS = 256


MASK_FILL = -1e30


def passed_along(value, axis, steps):
    count = lax.axis_size(axis)
    first, last = (max(0, -steps), min(count, count - steps))
    return lax.ppermute(value, axis, [(source, source + steps) for source in range(first, last)])


def lifted(row_data):
    return lax.optimization_barrier(row_data).astype(jnp.float32)


def doc_index(doc_lengths, first_place, row_count):
    doc_ends = jnp.cumsum(doc_lengths) * BLK
    places = first_place + jnp.arange(row_count, dtype=jnp.int32)
    labels = jnp.sum((places[:, None] >= doc_ends[None, :]).astype(jnp.int32), axis=1)
    return jnp.where(places < 0, -1, labels)


def widen_heads(row_data, copies):
    tokens_here = row_data.shape[0]
    head_count = row_data.shape[1] // HD
    shaped = row_data.reshape(tokens_here, head_count, 1, HD)
    shaped = jnp.broadcast_to(shaped, (tokens_here, head_count, copies, HD))
    return shaped.reshape(tokens_here, head_count * copies * HD)


def block_pass(q_block, g_block, k_win, v_win, allowed, score_scale):
    scores = (
        jnp.einsum("qhd,kd->hqk", q_block, k_win, preferred_element_type=jnp.float32)
        * score_scale
    )
    scores = jnp.where(allowed[None], scores, MASK_FILL)
    highest = jnp.max(scores, axis=-1, keepdims=True)
    row_total = jnp.sum(jnp.exp(scores - highest), axis=-1, keepdims=True)
    log_total = highest + jnp.log(row_total)
    weights = jnp.exp(scores - log_total)
    probs_bf = weights.astype(jnp.bfloat16)
    attn_block = jnp.einsum(
        "hqk,kd->qhd", probs_bf, v_win, preferred_element_type=jnp.float32
    ).astype(jnp.bfloat16)
    row_delta = jnp.transpose(jnp.sum(lifted(g_block) * lifted(attn_block), axis=-1), (1, 0))
    dprobs = jnp.einsum("qhd,kd->hqk", g_block, v_win, preferred_element_type=jnp.float32)
    dscores = (weights * (dprobs - row_delta[..., None])).astype(jnp.bfloat16)
    dq_block = (
        jnp.einsum("hqk,kd->qhd", dscores, k_win, preferred_element_type=jnp.float32)
        * score_scale
    ).astype(jnp.bfloat16)
    grad_k = jnp.einsum("hqk,qhd->kd", dscores, q_block, preferred_element_type=jnp.float32)
    grad_v = jnp.einsum("hqk,qhd->kd", probs_bf, g_block, preferred_element_type=jnp.float32)
    return attn_block, dq_block, grad_k, grad_v


def local(queries, key_rows, value_rows, out_grad, doc_lengths):
    seq_width = lax.axis_size("sp")
    tok_dev = queries.shape[0]
    span_rows = tok_dev * seq_width
    heads_q = queries.shape[1] // HD
    heads_k = key_rows.shape[1] // HD
    local_q = heads_q // seq_width
    copies = seq_width // heads_k
    score_scale = 1.0 / math.sqrt(HD)
    kv_pack = jnp.concatenate(
        [
            widen_heads(key_rows, copies).reshape(tok_dev, seq_width, HD),
            widen_heads(value_rows, copies).reshape(tok_dev, seq_width, HD),
        ],
        axis=2,
    )
    kv_seq = lax.all_to_all(kv_pack, "sp", split_axis=1, concat_axis=0, tiled=True)
    kv_seq = kv_seq.reshape(span_rows, 2 * HD)
    q_width = local_q * HD
    qg_pack = jnp.concatenate(
        [
            queries.reshape(tok_dev, seq_width, q_width),
            out_grad.reshape(tok_dev, seq_width, q_width),
        ],
        axis=2,
    )
    qg_seq = lax.all_to_all(qg_pack, "sp", split_axis=1, concat_axis=0, tiled=True)
    qg_seq = qg_seq.reshape(span_rows, 2 * q_width)
    q_seq = qg_seq[:, :q_width]
    g_seq = qg_seq[:, q_width:]
    reach = MOST_BLK * BLK
    reach_groups = (reach - 1) // span_rows + 1
    first_place = lax.axis_index("fsdp") * span_rows
    core = lax.axis_index("sp") % 2
    half = span_rows // 2
    sibling = [(s, s ^ 1) for s in range(seq_width)]
    my_half = lax.dynamic_slice_in_dim(kv_seq, core * half, half, 0)
    received = [passed_along(my_half, "fsdp", d) for d in range(reach_groups, 0, -1)]
    swapped = lax.ppermute(jnp.concatenate(received, axis=0), "sp", sibling)
    earlier = []
    for index, mine in enumerate(received):
        theirs = swapped[index * half : (index + 1) * half]
        earlier.append(
            jnp.where(
                core == 0,
                jnp.concatenate([mine, theirs], axis=0),
                jnp.concatenate([theirs, mine], axis=0),
            )
        )
    kv_all = jnp.concatenate(earlier + [kv_seq], axis=0)
    k_all = kv_all[:, :HD]
    v_all = kv_all[:, HD:]
    base_place = first_place - reach_groups * span_rows
    key_count = (reach_groups + 1) * span_rows
    labels = doc_index(doc_lengths, base_place, key_count)
    places = base_place + jnp.arange(key_count, dtype=jnp.int32)
    window = reach + Q_ROWS
    own_start = reach_groups * span_rows
    grad_k_all = jnp.zeros((key_count, HD), jnp.float32)
    grad_v_all = jnp.zeros((key_count, HD), jnp.float32)
    attn_parts, dq_parts = [], []
    for block in range(span_rows // Q_ROWS):
        q_lo = block * Q_ROWS
        k_lo = own_start + q_lo + Q_ROWS - window
        q_label = labels[own_start + q_lo : own_start + q_lo + Q_ROWS]
        q_place = places[own_start + q_lo : own_start + q_lo + Q_ROWS]
        k_label = labels[k_lo : k_lo + window]
        k_place = places[k_lo : k_lo + window]
        allowed = (q_label[:, None] == k_label[None, :]) & (k_place[None, :] <= q_place[:, None])
        q_block = q_seq[q_lo : q_lo + Q_ROWS].reshape(Q_ROWS, local_q, HD)
        g_block = g_seq[q_lo : q_lo + Q_ROWS].reshape(Q_ROWS, local_q, HD)
        attn_block, dq_block, grad_k, grad_v = block_pass(
            q_block,
            g_block,
            k_all[k_lo : k_lo + window],
            v_all[k_lo : k_lo + window],
            allowed,
            score_scale,
        )
        attn_parts.append(attn_block.reshape(Q_ROWS, local_q * HD))
        dq_parts.append(dq_block.reshape(Q_ROWS, local_q * HD))
        grad_k_all = grad_k_all.at[k_lo : k_lo + window].add(grad_k)
        grad_v_all = grad_v_all.at[k_lo : k_lo + window].add(grad_v)
    grad_kv_all = jnp.concatenate([grad_k_all, grad_v_all], axis=1)
    low_rows = jnp.stack(
        [grad_kv_all[g * span_rows : g * span_rows + half] for g in range(reach_groups)]
    )
    high_rows = jnp.stack(
        [grad_kv_all[g * span_rows + half : (g + 1) * span_rows] for g in range(reach_groups)]
    )
    mine_part = jnp.where(core == 0, low_rows, high_rows)
    their_part = jnp.where(core == 0, high_rows, low_rows)
    pair_sum = mine_part + lax.ppermute(their_part, "sp", sibling)
    backs = [
        passed_along(pair_sum[reach_groups - d].astype(jnp.bfloat16), "fsdp", -d)
        for d in range(1, reach_groups + 1)
    ]
    attn_seq = jnp.concatenate(attn_parts, axis=0)
    dq_seq = jnp.concatenate(dq_parts, axis=0)
    outgoing = jnp.concatenate([attn_seq, dq_seq], axis=1)
    back_all = lax.all_to_all(outgoing, "sp", split_axis=0, concat_axis=1, tiled=True)
    back_all = back_all.reshape(tok_dev, seq_width, outgoing.shape[1])
    attn_out = back_all[:, :, :q_width].reshape(tok_dev, heads_q * HD)
    grad_queries = back_all[:, :, q_width:].reshape(tok_dev, heads_q * HD)
    back_half = backs[0].astype(jnp.float32)
    for back in backs[1:]:
        back_half = back_half + back
    kv_sum = grad_kv_all[own_start:]
    kv_sum = lax.dynamic_update_slice_in_dim(
        kv_sum, lax.dynamic_slice_in_dim(kv_sum, core * half, half, 0) + back_half, core * half, 0
    )
    kv_sum = jnp.concatenate([kv_sum[:, :HD] * score_scale, kv_sum[:, HD:]], axis=1)
    kv_back = lax.all_to_all(
        kv_sum.astype(jnp.bfloat16), "sp", split_axis=0, concat_axis=1, tiled=True
    )
    kv_back = kv_back.reshape(tok_dev, seq_width, 2 * HD).astype(jnp.float32)
    grad_keys = jnp.sum(
        kv_back[:, :, :HD].reshape(tok_dev, heads_k, copies, HD), axis=2
    ).reshape(tok_dev, heads_k * HD)
    grad_values = jnp.sum(
        kv_back[:, :, HD:].reshape(tok_dev, heads_k, copies, HD), axis=2
    ).reshape(tok_dev, heads_k * HD)
    return (
        attn_out,
        grad_queries,
        grad_keys.astype(jnp.bfloat16),
        grad_values.astype(jnp.bfloat16),
    )


def solution(mesh):
    in_specs = (
        P(("fsdp", "sp"), None),
        P(("fsdp", "sp"), None),
        P(("fsdp", "sp"), None),
        P(("fsdp", "sp"), None),
        P(),
    )
    out_specs = (
        P(("fsdp", "sp"), None),
        P(("fsdp", "sp"), None),
        P(("fsdp", "sp"), None),
        P(("fsdp", "sp"), None),
    )
    return jax.shard_map(local, mesh=mesh, in_specs=in_specs, out_specs=out_specs, check_vma=False)
```

```python
import math

import jax
import jax.numpy as jnp
from jax import lax
from jax.sharding import PartitionSpec as P

HD = 128
BLK = 128
MOST_BLK = 16
Q_ROWS = 256


MASK_FILL = -1e30


def passed_along(value, axis, steps):
    count = lax.axis_size(axis)
    first, last = (max(0, -steps), min(count, count - steps))
    return lax.ppermute(value, axis, [(source, source + steps) for source in range(first, last)])


def lifted(row_data):
    return lax.optimization_barrier(row_data).astype(jnp.float32)


def doc_index(doc_lengths, first_place, row_count):
    doc_ends = jnp.cumsum(doc_lengths) * BLK
    places = first_place + jnp.arange(row_count, dtype=jnp.int32)
    labels = jnp.sum((places[:, None] >= doc_ends[None, :]).astype(jnp.int32), axis=1)
    return jnp.where(places < 0, -1, labels)


def widen_heads(row_data, copies):
    tokens_here = row_data.shape[0]
    head_count = row_data.shape[1] // HD
    shaped = row_data.reshape(tokens_here, head_count, 1, HD)
    shaped = jnp.broadcast_to(shaped, (tokens_here, head_count, copies, HD))
    return shaped.reshape(tokens_here, head_count * copies * HD)


def forward_pass(q_block, k_win, v_win, allowed, score_scale):
    scores = (
        jnp.einsum("qhd,kd->hqk", q_block, k_win, preferred_element_type=jnp.float32)
        * score_scale
    )
    scores = jnp.where(allowed[None], scores, MASK_FILL)
    highest = jnp.max(scores, axis=-1, keepdims=True)
    row_total = jnp.sum(jnp.exp(scores - highest), axis=-1, keepdims=True)
    log_total = highest + jnp.log(row_total)
    weights = jnp.exp(scores - log_total)
    probs_bf = weights.astype(jnp.bfloat16)
    attn_block = jnp.einsum(
        "hqk,kd->qhd", probs_bf, v_win, preferred_element_type=jnp.float32
    ).astype(jnp.bfloat16)
    return weights, probs_bf, attn_block


def backward_pass(q_block, g_block, k_win, v_win, weights, probs_bf, attn_block, score_scale):
    row_delta = jnp.transpose(jnp.sum(lifted(g_block) * lifted(attn_block), axis=-1), (1, 0))
    dprobs = jnp.einsum("qhd,kd->hqk", g_block, v_win, preferred_element_type=jnp.float32)
    dscores = (weights * (dprobs - row_delta[..., None])).astype(jnp.bfloat16)
    dq_block = (
        jnp.einsum("hqk,kd->qhd", dscores, k_win, preferred_element_type=jnp.float32)
        * score_scale
    ).astype(jnp.bfloat16)
    grad_k = jnp.einsum("hqk,qhd->kd", dscores, q_block, preferred_element_type=jnp.float32)
    grad_v = jnp.einsum("hqk,qhd->kd", probs_bf, g_block, preferred_element_type=jnp.float32)
    return dq_block, grad_k, grad_v


def local(queries, key_rows, value_rows, out_grad, doc_lengths):
    seq_width = lax.axis_size("sp")
    tok_dev = queries.shape[0]
    span_rows = tok_dev * seq_width
    heads_q = queries.shape[1] // HD
    heads_k = key_rows.shape[1] // HD
    local_q = heads_q // seq_width
    copies = seq_width // heads_k
    score_scale = 1.0 / math.sqrt(HD)
    kv_pack = jnp.concatenate(
        [
            widen_heads(key_rows, copies).reshape(tok_dev, seq_width, HD),
            widen_heads(value_rows, copies).reshape(tok_dev, seq_width, HD),
        ],
        axis=2,
    )
    kv_seq = lax.all_to_all(kv_pack, "sp", split_axis=1, concat_axis=0, tiled=True)
    kv_seq = kv_seq.reshape(span_rows, 2 * HD)
    q_width = local_q * HD
    q_seq = lax.all_to_all(
        queries.reshape(tok_dev, seq_width, q_width), "sp", split_axis=1, concat_axis=0, tiled=True
    ).reshape(span_rows, q_width)
    reach = MOST_BLK * BLK
    reach_groups = (reach - 1) // span_rows + 1
    first_place = lax.axis_index("fsdp") * span_rows
    core = lax.axis_index("sp") % 2
    half = span_rows // 2
    sibling = [(s, s ^ 1) for s in range(seq_width)]
    my_half = lax.dynamic_slice_in_dim(kv_seq, core * half, half, 0)
    received = [passed_along(my_half, "fsdp", d) for d in range(reach_groups, 0, -1)]
    swapped = lax.ppermute(jnp.concatenate(received, axis=0), "sp", sibling)
    earlier = []
    for index, mine in enumerate(received):
        theirs = swapped[index * half : (index + 1) * half]
        earlier.append(
            jnp.where(
                core == 0,
                jnp.concatenate([mine, theirs], axis=0),
                jnp.concatenate([theirs, mine], axis=0),
            )
        )
    kv_all = jnp.concatenate(earlier + [kv_seq], axis=0)
    q_seq, kv_all, g_pack = lax.optimization_barrier(
        (q_seq, kv_all, out_grad.reshape(tok_dev, seq_width, q_width))
    )
    g_seq = lax.all_to_all(g_pack, "sp", split_axis=1, concat_axis=0, tiled=True)
    g_seq = g_seq.reshape(span_rows, q_width)
    k_all = kv_all[:, :HD]
    v_all = kv_all[:, HD:]
    base_place = first_place - reach_groups * span_rows
    key_count = (reach_groups + 1) * span_rows
    labels = doc_index(doc_lengths, base_place, key_count)
    places = base_place + jnp.arange(key_count, dtype=jnp.int32)
    window = reach + Q_ROWS
    own_start = reach_groups * span_rows
    grad_k_all = jnp.zeros((key_count, HD), jnp.float32)
    grad_v_all = jnp.zeros((key_count, HD), jnp.float32)
    block_inputs = []
    for block in range(span_rows // Q_ROWS):
        q_lo = block * Q_ROWS
        k_lo = own_start + q_lo + Q_ROWS - window
        q_label = labels[own_start + q_lo : own_start + q_lo + Q_ROWS]
        q_place = places[own_start + q_lo : own_start + q_lo + Q_ROWS]
        k_label = labels[k_lo : k_lo + window]
        k_place = places[k_lo : k_lo + window]
        allowed = (q_label[:, None] == k_label[None, :]) & (k_place[None, :] <= q_place[:, None])
        q_block = q_seq[q_lo : q_lo + Q_ROWS].reshape(Q_ROWS, local_q, HD)
        block_inputs.append(
            (q_lo, k_lo, q_block, k_all[k_lo : k_lo + window], v_all[k_lo : k_lo + window], allowed)
        )
    forward_parts = [
        forward_pass(q_block, k_win, v_win, allowed, score_scale)
        for _, _, q_block, k_win, v_win, allowed in block_inputs
    ]
    attn_seq = jnp.concatenate(
        [attn.reshape(Q_ROWS, q_width) for _, _, attn in forward_parts], axis=0
    )
    attn_out = lax.all_to_all(attn_seq, "sp", split_axis=0, concat_axis=1, tiled=True)
    attn_out = attn_out.reshape(tok_dev, heads_q * HD)
    dq_parts = []
    for (q_lo, k_lo, q_block, k_win, v_win, _), (weights, probs_bf, attn) in zip(
        block_inputs, forward_parts
    ):
        g_block = g_seq[q_lo : q_lo + Q_ROWS].reshape(Q_ROWS, local_q, HD)
        dq_block, grad_k, grad_v = backward_pass(
            q_block, g_block, k_win, v_win, weights, probs_bf, attn, score_scale
        )
        dq_parts.append(dq_block.reshape(Q_ROWS, q_width))
        grad_k_all = grad_k_all.at[k_lo : k_lo + window].add(grad_k)
        grad_v_all = grad_v_all.at[k_lo : k_lo + window].add(grad_v)
    grad_kv_all = jnp.concatenate([grad_k_all, grad_v_all], axis=1)
    low_rows = jnp.stack(
        [grad_kv_all[g * span_rows : g * span_rows + half] for g in range(reach_groups)]
    )
    high_rows = jnp.stack(
        [grad_kv_all[g * span_rows + half : (g + 1) * span_rows] for g in range(reach_groups)]
    )
    mine_part = jnp.where(core == 0, low_rows, high_rows)
    their_part = jnp.where(core == 0, high_rows, low_rows)
    pair_sum = mine_part + lax.ppermute(their_part, "sp", sibling)
    backs = [
        passed_along(pair_sum[reach_groups - d].astype(jnp.bfloat16), "fsdp", -d)
        for d in range(1, reach_groups + 1)
    ]
    dq_seq = jnp.concatenate(dq_parts, axis=0)
    grad_queries = lax.all_to_all(dq_seq, "sp", split_axis=0, concat_axis=1, tiled=True)
    grad_queries = grad_queries.reshape(tok_dev, heads_q * HD)
    back_half = backs[0].astype(jnp.float32)
    for back in backs[1:]:
        back_half = back_half + back
    kv_sum = grad_kv_all[own_start:]
    kv_sum = lax.dynamic_update_slice_in_dim(
        kv_sum, lax.dynamic_slice_in_dim(kv_sum, core * half, half, 0) + back_half, core * half, 0
    )
    kv_sum = jnp.concatenate([kv_sum[:, :HD] * score_scale, kv_sum[:, HD:]], axis=1)
    kv_back = lax.all_to_all(
        kv_sum.astype(jnp.bfloat16), "sp", split_axis=0, concat_axis=1, tiled=True
    )
    kv_back = kv_back.reshape(tok_dev, seq_width, 2 * HD).astype(jnp.float32)
    grad_keys = jnp.sum(
        kv_back[:, :, :HD].reshape(tok_dev, heads_k, copies, HD), axis=2
    ).reshape(tok_dev, heads_k * HD)
    grad_values = jnp.sum(
        kv_back[:, :, HD:].reshape(tok_dev, heads_k, copies, HD), axis=2
    ).reshape(tok_dev, heads_k * HD)
    return (
        attn_out,
        grad_queries,
        grad_keys.astype(jnp.bfloat16),
        grad_values.astype(jnp.bfloat16),
    )


def solution(mesh):
    in_specs = (
        P(("fsdp", "sp"), None),
        P(("fsdp", "sp"), None),
        P(("fsdp", "sp"), None),
        P(("fsdp", "sp"), None),
        P(),
    )
    out_specs = (
        P(("fsdp", "sp"), None),
        P(("fsdp", "sp"), None),
        P(("fsdp", "sp"), None),
        P(("fsdp", "sp"), None),
    )
    return jax.shard_map(local, mesh=mesh, in_specs=in_specs, out_specs=out_specs, check_vma=False)
```

```python
import math

import jax
import jax.numpy as jnp
from jax import lax
from jax.sharding import PartitionSpec as P

HD = 128
BLK = 128
MOST_BLK = 16
Q_ROWS = 256


MASK_FILL = -1e30


def passed_along(value, axis, steps):
    count = lax.axis_size(axis)
    first, last = (max(0, -steps), min(count, count - steps))
    return lax.ppermute(value, axis, [(source, source + steps) for source in range(first, last)])


def lifted(row_data):
    return lax.optimization_barrier(row_data).astype(jnp.float32)


def doc_index(doc_lengths, first_place, row_count):
    doc_ends = jnp.cumsum(doc_lengths) * BLK
    places = first_place + jnp.arange(row_count, dtype=jnp.int32)
    labels = jnp.sum((places[:, None] >= doc_ends[None, :]).astype(jnp.int32), axis=1)
    return jnp.where(places < 0, -1, labels)


def widen_heads(row_data, copies):
    tokens_here = row_data.shape[0]
    head_count = row_data.shape[1] // HD
    shaped = row_data.reshape(tokens_here, head_count, 1, HD)
    shaped = jnp.broadcast_to(shaped, (tokens_here, head_count, copies, HD))
    return shaped.reshape(tokens_here, head_count * copies * HD)


def block_pass(q_block, g_block, k_win, v_win, allowed, score_scale):
    scores = (
        jnp.einsum("qhd,kd->hqk", q_block, k_win, preferred_element_type=jnp.float32)
        * score_scale
    )
    scores = jnp.where(allowed[None], scores, MASK_FILL)
    highest = jnp.max(scores, axis=-1, keepdims=True)
    row_total = jnp.sum(jnp.exp(scores - highest), axis=-1, keepdims=True)
    log_total = highest + jnp.log(row_total)
    weights = jnp.exp(scores - log_total)
    probs_bf = weights.astype(jnp.bfloat16)
    attn_block = jnp.einsum(
        "hqk,kd->qhd", probs_bf, v_win, preferred_element_type=jnp.float32
    ).astype(jnp.bfloat16)
    row_delta = jnp.transpose(jnp.sum(lifted(g_block) * lifted(attn_block), axis=-1), (1, 0))
    dprobs = jnp.einsum("qhd,kd->hqk", g_block, v_win, preferred_element_type=jnp.float32)
    dscores = (weights * (dprobs - row_delta[..., None])).astype(jnp.bfloat16)
    dq_block = (
        jnp.einsum("hqk,kd->qhd", dscores, k_win, preferred_element_type=jnp.float32)
        * score_scale
    ).astype(jnp.bfloat16)
    grad_k = jnp.einsum("hqk,qhd->kd", dscores, q_block, preferred_element_type=jnp.float32)
    grad_v = jnp.einsum("hqk,qhd->kd", probs_bf, g_block, preferred_element_type=jnp.float32)
    return attn_block, dq_block, grad_k, grad_v


def local(queries, key_rows, value_rows, out_grad, doc_lengths):
    seq_width = lax.axis_size("sp")
    tok_dev = queries.shape[0]
    span_rows = tok_dev * seq_width
    heads_q = queries.shape[1] // HD
    heads_k = key_rows.shape[1] // HD
    local_q = heads_q // seq_width
    copies = seq_width // heads_k
    score_scale = 1.0 / math.sqrt(HD)
    core = lax.axis_index("sp") % 2
    sibling = [(s, s ^ 1) for s in range(seq_width)]
    part_rows = tok_dev // 2
    kv_heads = jnp.concatenate(
        [key_rows.reshape(tok_dev, heads_k, HD), value_rows.reshape(tok_dev, heads_k, HD)],
        axis=2,
    )
    kv_send = jnp.transpose(kv_heads.reshape(2, part_rows, heads_k, 2 * HD), (2, 0, 1, 3))
    kv_send = kv_send.reshape(seq_width, part_rows, 2 * HD)
    kv_mine = lax.all_to_all(kv_send, "sp", split_axis=0, concat_axis=0, tiled=True)

    def joined(mine, theirs):
        return jnp.where(
            core == 0, jnp.stack([mine, theirs], axis=1), jnp.stack([theirs, mine], axis=1)
        ).reshape(span_rows, 2 * HD)

    q_width = local_q * HD
    qg_pack = jnp.concatenate(
        [
            queries.reshape(tok_dev, seq_width, q_width),
            out_grad.reshape(tok_dev, seq_width, q_width),
        ],
        axis=2,
    )
    qg_seq = lax.all_to_all(qg_pack, "sp", split_axis=1, concat_axis=0, tiled=True)
    qg_seq = qg_seq.reshape(span_rows, 2 * q_width)
    q_seq = qg_seq[:, :q_width]
    g_seq = qg_seq[:, q_width:]
    reach = MOST_BLK * BLK
    reach_groups = (reach - 1) // span_rows + 1
    first_place = lax.axis_index("fsdp") * span_rows
    received = [passed_along(kv_mine, "fsdp", d) for d in range(reach_groups, 0, -1)]
    own_theirs = lax.ppermute(kv_mine, "sp", sibling)
    swapped = lax.ppermute(jnp.stack(received), "sp", sibling)
    earlier = [joined(mine, swapped[index]) for index, mine in enumerate(received)]
    kv_all = jnp.concatenate(earlier + [joined(kv_mine, own_theirs)], axis=0)
    k_all = kv_all[:, :HD]
    v_all = kv_all[:, HD:]
    base_place = first_place - reach_groups * span_rows
    key_count = (reach_groups + 1) * span_rows
    labels = doc_index(doc_lengths, base_place, key_count)
    places = base_place + jnp.arange(key_count, dtype=jnp.int32)
    window = reach + Q_ROWS
    own_start = reach_groups * span_rows
    grad_k_all = jnp.zeros((key_count, HD), jnp.float32)
    grad_v_all = jnp.zeros((key_count, HD), jnp.float32)
    attn_parts, dq_parts = [], []
    for block in range(span_rows // Q_ROWS):
        q_lo = block * Q_ROWS
        k_lo = own_start + q_lo + Q_ROWS - window
        q_label = labels[own_start + q_lo : own_start + q_lo + Q_ROWS]
        q_place = places[own_start + q_lo : own_start + q_lo + Q_ROWS]
        k_label = labels[k_lo : k_lo + window]
        k_place = places[k_lo : k_lo + window]
        allowed = (q_label[:, None] == k_label[None, :]) & (k_place[None, :] <= q_place[:, None])
        q_block = q_seq[q_lo : q_lo + Q_ROWS].reshape(Q_ROWS, local_q, HD)
        g_block = g_seq[q_lo : q_lo + Q_ROWS].reshape(Q_ROWS, local_q, HD)
        attn_block, dq_block, grad_k, grad_v = block_pass(
            q_block,
            g_block,
            k_all[k_lo : k_lo + window],
            v_all[k_lo : k_lo + window],
            allowed,
            score_scale,
        )
        attn_parts.append(attn_block.reshape(Q_ROWS, local_q * HD))
        dq_parts.append(dq_block.reshape(Q_ROWS, local_q * HD))
        grad_k_all = grad_k_all.at[k_lo : k_lo + window].add(grad_k)
        grad_v_all = grad_v_all.at[k_lo : k_lo + window].add(grad_v)
    grad_kv_all = jnp.concatenate([grad_k_all, grad_v_all], axis=1)
    grad_parts = grad_kv_all.reshape(reach_groups + 1, seq_width, 2, part_rows, 2 * HD)
    low_rows = grad_parts[:, :, 0]
    high_rows = grad_parts[:, :, 1]
    mine_part = jnp.where(core == 0, low_rows, high_rows)
    their_part = jnp.where(core == 0, high_rows, low_rows)
    pair_sum = mine_part + lax.ppermute(their_part, "sp", sibling)
    backs = [
        passed_along(pair_sum[reach_groups - d].astype(jnp.bfloat16), "fsdp", -d)
        for d in range(1, reach_groups + 1)
    ]
    attn_seq = jnp.concatenate(attn_parts, axis=0)
    dq_seq = jnp.concatenate(dq_parts, axis=0)
    outgoing = jnp.concatenate([attn_seq, dq_seq], axis=1)
    back_all = lax.all_to_all(outgoing, "sp", split_axis=0, concat_axis=1, tiled=True)
    back_all = back_all.reshape(tok_dev, seq_width, outgoing.shape[1])
    attn_out = back_all[:, :, :q_width].reshape(tok_dev, heads_q * HD)
    grad_queries = back_all[:, :, q_width:].reshape(tok_dev, heads_q * HD)
    kv_sum = pair_sum[reach_groups]
    for back in backs:
        kv_sum = kv_sum + back
    kv_sum = jnp.concatenate([kv_sum[..., :HD] * score_scale, kv_sum[..., HD:]], axis=-1)
    kv_back = lax.all_to_all(
        kv_sum.astype(jnp.bfloat16), "sp", split_axis=0, concat_axis=0, tiled=True
    )
    kv_back = jnp.transpose(
        kv_back.reshape(heads_k, 2, part_rows, 2 * HD), (1, 2, 0, 3)
    ).reshape(tok_dev, heads_k, 2 * HD)
    grad_keys = kv_back[:, :, :HD].reshape(tok_dev, heads_k * HD)
    grad_values = kv_back[:, :, HD:].reshape(tok_dev, heads_k * HD)
    return (
        attn_out,
        grad_queries,
        grad_keys.astype(jnp.bfloat16),
        grad_values.astype(jnp.bfloat16),
    )


def solution(mesh):
    in_specs = (
        P(("fsdp", "sp"), None),
        P(("fsdp", "sp"), None),
        P(("fsdp", "sp"), None),
        P(("fsdp", "sp"), None),
        P(),
    )
    out_specs = (
        P(("fsdp", "sp"), None),
        P(("fsdp", "sp"), None),
        P(("fsdp", "sp"), None),
        P(("fsdp", "sp"), None),
    )
    return jax.shard_map(local, mesh=mesh, in_specs=in_specs, out_specs=out_specs, check_vma=False)
```

```python
import math

import jax
import jax.numpy as jnp
from jax import lax
from jax.sharding import PartitionSpec as P

HD = 128
BLK = 128
MOST_BLK = 16
Q_ROWS = 256


MASK_FILL = -1e30


def passed_along(value, axis, steps):
    count = lax.axis_size(axis)
    first, last = (max(0, -steps), min(count, count - steps))
    return lax.ppermute(value, axis, [(source, source + steps) for source in range(first, last)])


def lifted(row_data):
    return lax.optimization_barrier(row_data).astype(jnp.float32)


def doc_index(doc_lengths, first_place, row_count):
    doc_ends = jnp.cumsum(doc_lengths) * BLK
    places = first_place + jnp.arange(row_count, dtype=jnp.int32)
    labels = jnp.sum((places[:, None] >= doc_ends[None, :]).astype(jnp.int32), axis=1)
    return jnp.where(places < 0, -1, labels)


def widen_heads(row_data, copies):
    tokens_here = row_data.shape[0]
    head_count = row_data.shape[1] // HD
    shaped = row_data.reshape(tokens_here, head_count, 1, HD)
    shaped = jnp.broadcast_to(shaped, (tokens_here, head_count, copies, HD))
    return shaped.reshape(tokens_here, head_count * copies * HD)


def block_pass(q_block, g_block, k_win, v_win, allowed, score_scale):
    scores = (
        jnp.einsum("qhd,kd->hqk", q_block, k_win, preferred_element_type=jnp.float32)
        * score_scale
    )
    scores = jnp.where(allowed[None], scores, MASK_FILL)
    highest = jnp.max(scores, axis=-1, keepdims=True)
    row_total = jnp.sum(jnp.exp(scores - highest), axis=-1, keepdims=True)
    log_total = highest + jnp.log(row_total)
    weights = jnp.exp(scores - log_total)
    probs_bf = weights.astype(jnp.bfloat16)
    attn_block = jnp.einsum(
        "hqk,kd->qhd", probs_bf, v_win, preferred_element_type=jnp.float32
    ).astype(jnp.bfloat16)
    row_delta = jnp.transpose(jnp.sum(lifted(g_block) * lifted(attn_block), axis=-1), (1, 0))
    dprobs = jnp.einsum("qhd,kd->hqk", g_block, v_win, preferred_element_type=jnp.float32)
    dscores = (weights * (dprobs - row_delta[..., None])).astype(jnp.bfloat16)
    dq_block = (
        jnp.einsum("hqk,kd->qhd", dscores, k_win, preferred_element_type=jnp.float32)
        * score_scale
    ).astype(jnp.bfloat16)
    grad_k = jnp.einsum("hqk,qhd->kd", dscores, q_block, preferred_element_type=jnp.float32)
    grad_v = jnp.einsum("hqk,qhd->kd", probs_bf, g_block, preferred_element_type=jnp.float32)
    return attn_block, dq_block, grad_k, grad_v


def local(queries, key_rows, value_rows, out_grad, doc_lengths):
    seq_width = lax.axis_size("sp")
    tok_dev = queries.shape[0]
    span_rows = tok_dev * seq_width
    heads_q = queries.shape[1] // HD
    heads_k = key_rows.shape[1] // HD
    local_q = heads_q // seq_width
    copies = seq_width // heads_k
    score_scale = 1.0 / math.sqrt(HD)
    core = lax.axis_index("sp") % 2
    sibling = [(s, s ^ 1) for s in range(seq_width)]
    part_rows = tok_dev // 2
    kv_heads = jnp.concatenate(
        [key_rows.reshape(tok_dev, heads_k, HD), value_rows.reshape(tok_dev, heads_k, HD)],
        axis=2,
    )
    kv_send = jnp.transpose(kv_heads.reshape(2, part_rows, heads_k, 2 * HD), (2, 0, 1, 3))
    kv_send = kv_send.reshape(seq_width, part_rows, 2 * HD)
    kv_mine = lax.all_to_all(kv_send, "sp", split_axis=0, concat_axis=0, tiled=True)

    def joined(mine, theirs):
        return jnp.where(
            core == 0, jnp.stack([mine, theirs], axis=1), jnp.stack([theirs, mine], axis=1)
        ).reshape(span_rows, 2 * HD)

    q_width = local_q * HD
    qg_pack = jnp.concatenate(
        [
            queries.reshape(tok_dev, seq_width, q_width),
            out_grad.reshape(tok_dev, seq_width, q_width),
        ],
        axis=2,
    )
    qg_seq = lax.all_to_all(qg_pack, "sp", split_axis=1, concat_axis=0, tiled=True)
    qg_seq = qg_seq.reshape(span_rows, 2 * q_width)
    q_seq = qg_seq[:, :q_width]
    g_seq = qg_seq[:, q_width:]
    reach = MOST_BLK * BLK
    reach_groups = (reach - 1) // span_rows + 1
    first_place = lax.axis_index("fsdp") * span_rows
    received = [passed_along(kv_mine, "fsdp", d) for d in range(reach_groups, 0, -1)]
    own_theirs = lax.ppermute(kv_mine, "sp", sibling)
    swapped = lax.ppermute(jnp.stack(received), "sp", sibling)
    earlier = [joined(mine, swapped[index]) for index, mine in enumerate(received)]
    kv_all = jnp.concatenate(earlier + [joined(kv_mine, own_theirs)], axis=0)
    k_all = kv_all[:, :HD]
    v_all = kv_all[:, HD:]
    base_place = first_place - reach_groups * span_rows
    key_count = (reach_groups + 1) * span_rows
    labels = doc_index(doc_lengths, base_place, key_count)
    places = base_place + jnp.arange(key_count, dtype=jnp.int32)
    window = reach + Q_ROWS
    own_start = reach_groups * span_rows
    grad_k_all = jnp.zeros((key_count, HD), jnp.float32)
    grad_v_all = jnp.zeros((key_count, HD), jnp.float32)
    attn_parts, dq_parts = [], []
    for block in range(span_rows // Q_ROWS):
        q_lo = block * Q_ROWS
        k_lo = own_start + q_lo + Q_ROWS - window
        q_label = labels[own_start + q_lo : own_start + q_lo + Q_ROWS]
        q_place = places[own_start + q_lo : own_start + q_lo + Q_ROWS]
        k_label = labels[k_lo : k_lo + window]
        k_place = places[k_lo : k_lo + window]
        allowed = (q_label[:, None] == k_label[None, :]) & (k_place[None, :] <= q_place[:, None])
        q_block = q_seq[q_lo : q_lo + Q_ROWS].reshape(Q_ROWS, local_q, HD)
        g_block = g_seq[q_lo : q_lo + Q_ROWS].reshape(Q_ROWS, local_q, HD)
        attn_block, dq_block, grad_k, grad_v = block_pass(
            q_block,
            g_block,
            k_all[k_lo : k_lo + window],
            v_all[k_lo : k_lo + window],
            allowed,
            score_scale,
        )
        attn_parts.append(attn_block.reshape(Q_ROWS, local_q * HD))
        dq_parts.append(dq_block.reshape(Q_ROWS, local_q * HD))
        grad_k_all = grad_k_all.at[k_lo : k_lo + window].add(grad_k)
        grad_v_all = grad_v_all.at[k_lo : k_lo + window].add(grad_v)
    grad_kv_all = jnp.concatenate([grad_k_all, grad_v_all], axis=1)
    half = span_rows // 2
    low_rows = jnp.stack(
        [grad_kv_all[g * span_rows : g * span_rows + half] for g in range(reach_groups)]
    )
    high_rows = jnp.stack(
        [grad_kv_all[g * span_rows + half : (g + 1) * span_rows] for g in range(reach_groups)]
    )
    mine_part = jnp.where(core == 0, low_rows, high_rows)
    their_part = jnp.where(core == 0, high_rows, low_rows)
    pair_sum = mine_part + lax.ppermute(their_part, "sp", sibling)
    backs = [
        passed_along(pair_sum[reach_groups - d].astype(jnp.bfloat16), "fsdp", -d)
        for d in range(1, reach_groups + 1)
    ]
    attn_seq = jnp.concatenate(attn_parts, axis=0)
    dq_seq = jnp.concatenate(dq_parts, axis=0)
    back_half = backs[0].astype(jnp.float32)
    for back in backs[1:]:
        back_half = back_half + back
    kv_sum = grad_kv_all[own_start:]
    kv_sum = lax.dynamic_update_slice_in_dim(
        kv_sum, lax.dynamic_slice_in_dim(kv_sum, core * half, half, 0) + back_half, core * half, 0
    )
    kv_sum = jnp.concatenate([kv_sum[:, :HD] * score_scale, kv_sum[:, HD:]], axis=1)
    outgoing = jnp.concatenate([attn_seq, dq_seq, kv_sum.astype(jnp.bfloat16)], axis=1)
    back_all = lax.all_to_all(outgoing, "sp", split_axis=0, concat_axis=1, tiled=True)
    back_all = back_all.reshape(tok_dev, seq_width, outgoing.shape[1])
    attn_out = back_all[:, :, :q_width].reshape(tok_dev, heads_q * HD)
    grad_queries = back_all[:, :, q_width : 2 * q_width].reshape(tok_dev, heads_q * HD)
    kv_back = back_all[:, :, 2 * q_width :].astype(jnp.float32)
    kv_back = jnp.sum(kv_back.reshape(tok_dev, heads_k, seq_width // heads_k, 2 * HD), axis=2)
    grad_keys = kv_back[:, :, :HD].reshape(tok_dev, heads_k * HD)
    grad_values = kv_back[:, :, HD:].reshape(tok_dev, heads_k * HD)
    return (
        attn_out,
        grad_queries,
        grad_keys.astype(jnp.bfloat16),
        grad_values.astype(jnp.bfloat16),
    )


def solution(mesh):
    in_specs = (
        P(("fsdp", "sp"), None),
        P(("fsdp", "sp"), None),
        P(("fsdp", "sp"), None),
        P(("fsdp", "sp"), None),
        P(),
    )
    out_specs = (
        P(("fsdp", "sp"), None),
        P(("fsdp", "sp"), None),
        P(("fsdp", "sp"), None),
        P(("fsdp", "sp"), None),
    )
    return jax.shard_map(local, mesh=mesh, in_specs=in_specs, out_specs=out_specs, check_vma=False)
```

```python
import math

import jax
import jax.numpy as jnp
from jax import lax
from jax.sharding import PartitionSpec as P

HD = 128
BLK = 128
MOST_BLK = 16
Q_ROWS = 256


MASK_FILL = -1e30


def passed_along(value, axis, steps):
    count = lax.axis_size(axis)
    first, last = (max(0, -steps), min(count, count - steps))
    return lax.ppermute(value, axis, [(source, source + steps) for source in range(first, last)])


def lifted(row_data):
    return lax.optimization_barrier(row_data).astype(jnp.float32)


def doc_index(doc_lengths, first_place, row_count):
    doc_ends = jnp.cumsum(doc_lengths) * BLK
    places = first_place + jnp.arange(row_count, dtype=jnp.int32)
    labels = jnp.sum((places[:, None] >= doc_ends[None, :]).astype(jnp.int32), axis=1)
    return jnp.where(places < 0, -1, labels)


def widen_heads(row_data, copies):
    tokens_here = row_data.shape[0]
    head_count = row_data.shape[1] // HD
    shaped = row_data.reshape(tokens_here, head_count, 1, HD)
    shaped = jnp.broadcast_to(shaped, (tokens_here, head_count, copies, HD))
    return shaped.reshape(tokens_here, head_count * copies * HD)


def block_pass(q_block, g_block, k_win, v_win, allowed, score_scale):
    scores = (
        jnp.einsum("qhd,kd->hqk", q_block, k_win, preferred_element_type=jnp.float32)
        * score_scale
    )
    scores = jnp.where(allowed[None], scores, MASK_FILL)
    highest = jnp.max(scores, axis=-1, keepdims=True)
    row_total = jnp.sum(jnp.exp(scores - highest), axis=-1, keepdims=True)
    log_total = highest + jnp.log(row_total)
    weights = jnp.exp(scores - log_total)
    probs_bf = weights.astype(jnp.bfloat16)
    attn_block = jnp.einsum(
        "hqk,kd->qhd", probs_bf, v_win, preferred_element_type=jnp.float32
    ).astype(jnp.bfloat16)
    row_delta = jnp.transpose(jnp.sum(lifted(g_block) * lifted(attn_block), axis=-1), (1, 0))
    dprobs = jnp.einsum("qhd,kd->hqk", g_block, v_win, preferred_element_type=jnp.float32)
    dscores = (weights * (dprobs - row_delta[..., None])).astype(jnp.bfloat16)
    dq_block = (
        jnp.einsum("hqk,kd->qhd", dscores, k_win, preferred_element_type=jnp.float32)
        * score_scale
    ).astype(jnp.bfloat16)
    grad_k = jnp.einsum("hqk,qhd->kd", dscores, q_block, preferred_element_type=jnp.float32)
    grad_v = jnp.einsum("hqk,qhd->kd", probs_bf, g_block, preferred_element_type=jnp.float32)
    return attn_block, dq_block, grad_k, grad_v


def local(queries, key_rows, value_rows, out_grad, doc_lengths):
    seq_width = lax.axis_size("sp")
    tok_dev = queries.shape[0]
    span_rows = tok_dev * seq_width
    heads_q = queries.shape[1] // HD
    heads_k = key_rows.shape[1] // HD
    local_q = heads_q // seq_width
    copies = seq_width // heads_k
    score_scale = 1.0 / math.sqrt(HD)
    core = lax.axis_index("sp") % 2
    sibling = [(s, s ^ 1) for s in range(seq_width)]
    part_rows = tok_dev // 2
    kv_heads = jnp.concatenate(
        [key_rows.reshape(tok_dev, heads_k, HD), value_rows.reshape(tok_dev, heads_k, HD)],
        axis=2,
    )
    kv_send = jnp.transpose(kv_heads.reshape(2, part_rows, heads_k, 2 * HD), (2, 0, 1, 3))
    kv_send = kv_send.reshape(seq_width, part_rows, 2 * HD)
    kv_mine = lax.all_to_all(kv_send, "sp", split_axis=0, concat_axis=0, tiled=True)

    def joined(mine, theirs):
        return jnp.where(
            core == 0, jnp.stack([mine, theirs], axis=1), jnp.stack([theirs, mine], axis=1)
        ).reshape(span_rows, 2 * HD)

    q_width = local_q * HD
    qg_pack = jnp.concatenate(
        [
            queries.reshape(tok_dev, seq_width, q_width),
            out_grad.reshape(tok_dev, seq_width, q_width),
        ],
        axis=2,
    )
    qg_seq = lax.all_to_all(qg_pack, "sp", split_axis=1, concat_axis=0, tiled=True)
    qg_seq = qg_seq.reshape(span_rows, 2 * q_width)
    q_seq = qg_seq[:, :q_width]
    g_seq = qg_seq[:, q_width:]
    reach = MOST_BLK * BLK
    reach_groups = (reach - 1) // span_rows + 1
    first_place = lax.axis_index("fsdp") * span_rows
    received = [passed_along(kv_mine, "fsdp", d) for d in range(reach_groups, 0, -1)]
    own_theirs = lax.ppermute(kv_mine, "sp", sibling)
    swapped = lax.ppermute(jnp.stack(received), "sp", sibling)
    earlier = [joined(mine, swapped[index]) for index, mine in enumerate(received)]
    kv_all = jnp.concatenate(earlier + [joined(kv_mine, own_theirs)], axis=0)
    k_all = kv_all[:, :HD]
    v_all = kv_all[:, HD:]
    base_place = first_place - reach_groups * span_rows
    key_count = (reach_groups + 1) * span_rows
    labels = doc_index(doc_lengths, base_place, key_count)
    places = base_place + jnp.arange(key_count, dtype=jnp.int32)
    window = reach + Q_ROWS
    own_start = reach_groups * span_rows
    grad_k_all = jnp.zeros((key_count, HD), jnp.float32)
    grad_v_all = jnp.zeros((key_count, HD), jnp.float32)
    attn_parts, dq_parts = [], []
    for block in range(span_rows // Q_ROWS):
        q_lo = block * Q_ROWS
        k_lo = own_start + q_lo + Q_ROWS - window
        q_label = labels[own_start + q_lo : own_start + q_lo + Q_ROWS]
        q_place = places[own_start + q_lo : own_start + q_lo + Q_ROWS]
        k_label = labels[k_lo : k_lo + window]
        k_place = places[k_lo : k_lo + window]
        allowed = (q_label[:, None] == k_label[None, :]) & (k_place[None, :] <= q_place[:, None])
        q_block = q_seq[q_lo : q_lo + Q_ROWS].reshape(Q_ROWS, local_q, HD)
        g_block = g_seq[q_lo : q_lo + Q_ROWS].reshape(Q_ROWS, local_q, HD)
        attn_block, dq_block, grad_k, grad_v = block_pass(
            q_block,
            g_block,
            k_all[k_lo : k_lo + window],
            v_all[k_lo : k_lo + window],
            allowed,
            score_scale,
        )
        attn_parts.append(attn_block.reshape(Q_ROWS, local_q * HD))
        dq_parts.append(dq_block.reshape(Q_ROWS, local_q * HD))
        grad_k_all = grad_k_all.at[k_lo : k_lo + window].add(grad_k)
        grad_v_all = grad_v_all.at[k_lo : k_lo + window].add(grad_v)
    grad_kv_all = jnp.concatenate([grad_k_all, grad_v_all], axis=1)
    half = span_rows // 2
    low_rows = jnp.stack(
        [grad_kv_all[g * span_rows : g * span_rows + half] for g in range(reach_groups)]
    )
    high_rows = jnp.stack(
        [grad_kv_all[g * span_rows + half : (g + 1) * span_rows] for g in range(reach_groups)]
    )
    mine_part = jnp.where(core == 0, low_rows, high_rows)
    their_part = jnp.where(core == 0, high_rows, low_rows)
    pair_sum = mine_part + lax.ppermute(their_part, "sp", sibling)
    backs = [
        passed_along(pair_sum[reach_groups - d].astype(jnp.bfloat16), "fsdp", -d)
        for d in range(1, reach_groups + 1)
    ]
    attn_seq = jnp.concatenate(attn_parts, axis=0)
    dq_seq = jnp.concatenate(dq_parts, axis=0)
    outgoing = jnp.concatenate([attn_seq, dq_seq], axis=1)
    back_all = lax.all_to_all(outgoing, "sp", split_axis=0, concat_axis=1, tiled=True)
    back_all = back_all.reshape(tok_dev, seq_width, outgoing.shape[1])
    attn_out = back_all[:, :, :q_width].reshape(tok_dev, heads_q * HD)
    grad_queries = back_all[:, :, q_width:].reshape(tok_dev, heads_q * HD)
    back_half = backs[0].astype(jnp.float32)
    for back in backs[1:]:
        back_half = back_half + back
    kv_sum = grad_kv_all[own_start:]
    kv_sum = lax.dynamic_update_slice_in_dim(
        kv_sum, lax.dynamic_slice_in_dim(kv_sum, core * half, half, 0) + back_half, core * half, 0
    )
    kv_sum = jnp.concatenate([kv_sum[:, :HD] * score_scale, kv_sum[:, HD:]], axis=1)
    kv_back = lax.all_to_all(
        kv_sum.astype(jnp.bfloat16), "sp", split_axis=0, concat_axis=1, tiled=True
    )
    kv_back = kv_back.reshape(tok_dev, seq_width, 2 * HD).astype(jnp.float32)
    kv_back = jnp.sum(kv_back.reshape(tok_dev, heads_k, seq_width // heads_k, 2 * HD), axis=2)
    grad_keys = kv_back[:, :, :HD].reshape(tok_dev, heads_k * HD)
    grad_values = kv_back[:, :, HD:].reshape(tok_dev, heads_k * HD)
    return (
        attn_out,
        grad_queries,
        grad_keys.astype(jnp.bfloat16),
        grad_values.astype(jnp.bfloat16),
    )


def solution(mesh):
    in_specs = (
        P(("fsdp", "sp"), None),
        P(("fsdp", "sp"), None),
        P(("fsdp", "sp"), None),
        P(("fsdp", "sp"), None),
        P(),
    )
    out_specs = (
        P(("fsdp", "sp"), None),
        P(("fsdp", "sp"), None),
        P(("fsdp", "sp"), None),
        P(("fsdp", "sp"), None),
    )
    return jax.shard_map(local, mesh=mesh, in_specs=in_specs, out_specs=out_specs, check_vma=False)
```

```python
import math

import jax
import jax.numpy as jnp
from jax import lax
from jax.sharding import PartitionSpec as P

HD = 128
BLK = 128
MOST_BLK = 16
Q_ROWS = 256


MASK_FILL = -1e30


def passed_along(value, axis, steps):
    count = lax.axis_size(axis)
    first, last = (max(0, -steps), min(count, count - steps))
    return lax.ppermute(value, axis, [(source, source + steps) for source in range(first, last)])


def lifted(row_data):
    return lax.optimization_barrier(row_data).astype(jnp.float32)


def doc_index(doc_lengths, first_place, row_count):
    doc_ends = jnp.cumsum(doc_lengths) * BLK
    places = first_place + jnp.arange(row_count, dtype=jnp.int32)
    labels = jnp.sum((places[:, None] >= doc_ends[None, :]).astype(jnp.int32), axis=1)
    return jnp.where(places < 0, -1, labels)


def widen_heads(row_data, copies):
    tokens_here = row_data.shape[0]
    head_count = row_data.shape[1] // HD
    shaped = row_data.reshape(tokens_here, head_count, 1, HD)
    shaped = jnp.broadcast_to(shaped, (tokens_here, head_count, copies, HD))
    return shaped.reshape(tokens_here, head_count * copies * HD)


def block_pass(q_block, g_block, k_win, v_win, allowed, score_scale):
    scores = (
        jnp.einsum("qhd,kd->hqk", q_block, k_win, preferred_element_type=jnp.float32)
        * score_scale
    )
    scores = jnp.where(allowed[None], scores, MASK_FILL)
    highest = jnp.max(scores, axis=-1, keepdims=True)
    row_total = jnp.sum(jnp.exp(scores - highest), axis=-1, keepdims=True)
    log_total = highest + jnp.log(row_total)
    weights = jnp.exp(scores - log_total)
    probs_bf = weights.astype(jnp.bfloat16)
    attn_block = jnp.einsum(
        "hqk,kd->qhd", probs_bf, v_win, preferred_element_type=jnp.float32
    ).astype(jnp.bfloat16)
    row_delta = jnp.transpose(jnp.sum(lifted(g_block) * lifted(attn_block), axis=-1), (1, 0))
    dprobs = jnp.einsum("qhd,kd->hqk", g_block, v_win, preferred_element_type=jnp.float32)
    dscores = (weights * (dprobs - row_delta[..., None])).astype(jnp.bfloat16)
    dq_block = (
        jnp.einsum("hqk,kd->qhd", dscores, k_win, preferred_element_type=jnp.float32)
        * score_scale
    ).astype(jnp.bfloat16)
    grad_k = jnp.einsum("hqk,qhd->kd", dscores, q_block, preferred_element_type=jnp.float32)
    grad_v = jnp.einsum("hqk,qhd->kd", probs_bf, g_block, preferred_element_type=jnp.float32)
    return attn_block, dq_block, grad_k, grad_v


def local(queries, key_rows, value_rows, out_grad, doc_lengths):
    seq_width = lax.axis_size("sp")
    tok_dev = queries.shape[0]
    span_rows = tok_dev * seq_width
    heads_q = queries.shape[1] // HD
    heads_k = key_rows.shape[1] // HD
    local_q = heads_q // seq_width
    copies = seq_width // heads_k
    score_scale = 1.0 / math.sqrt(HD)
    core = lax.axis_index("sp") % 2
    sibling = [(s, s ^ 1) for s in range(seq_width)]
    part_rows = tok_dev // 2
    kv_heads = jnp.concatenate(
        [key_rows.reshape(tok_dev, heads_k, HD), value_rows.reshape(tok_dev, heads_k, HD)],
        axis=2,
    )
    kv_send = jnp.transpose(kv_heads.reshape(2, part_rows, heads_k, 2 * HD), (2, 0, 1, 3))
    kv_send = kv_send.reshape(seq_width, part_rows, 2 * HD)
    kv_mine = lax.all_to_all(kv_send, "sp", split_axis=0, concat_axis=0, tiled=True)

    def joined(mine, theirs):
        return jnp.where(
            core == 0, jnp.stack([mine, theirs], axis=1), jnp.stack([theirs, mine], axis=1)
        ).reshape(span_rows, 2 * HD)

    q_width = local_q * HD
    qg_pack = jnp.concatenate(
        [
            queries.reshape(tok_dev, seq_width, q_width),
            out_grad.reshape(tok_dev, seq_width, q_width),
        ],
        axis=2,
    )
    qg_seq = lax.all_to_all(qg_pack, "sp", split_axis=1, concat_axis=0, tiled=True)
    qg_seq = qg_seq.reshape(span_rows, 2 * q_width)
    q_seq = qg_seq[:, :q_width]
    g_seq = qg_seq[:, q_width:]
    reach = MOST_BLK * BLK
    reach_groups = (reach - 1) // span_rows + 1
    first_place = lax.axis_index("fsdp") * span_rows
    received = [passed_along(kv_mine, "fsdp", d) for d in range(reach_groups, 0, -1)]
    own_theirs = lax.ppermute(kv_mine, "sp", sibling)
    swapped = lax.ppermute(jnp.stack(received), "sp", sibling)
    earlier = [joined(mine, swapped[index]) for index, mine in enumerate(received)]
    kv_all = jnp.concatenate(earlier + [joined(kv_mine, own_theirs)], axis=0)
    k_all = kv_all[:, :HD]
    v_all = kv_all[:, HD:]
    base_place = first_place - reach_groups * span_rows
    key_count = (reach_groups + 1) * span_rows
    labels = doc_index(doc_lengths, base_place, key_count)
    places = base_place + jnp.arange(key_count, dtype=jnp.int32)
    window = reach + Q_ROWS
    own_start = reach_groups * span_rows
    grad_k_all = jnp.zeros((key_count, HD), jnp.float32)
    grad_v_all = jnp.zeros((key_count, HD), jnp.float32)
    attn_parts, dq_parts = [], []
    for block in range(span_rows // Q_ROWS):
        q_lo = block * Q_ROWS
        k_lo = own_start + q_lo + Q_ROWS - window
        q_label = labels[own_start + q_lo : own_start + q_lo + Q_ROWS]
        q_place = places[own_start + q_lo : own_start + q_lo + Q_ROWS]
        k_label = labels[k_lo : k_lo + window]
        k_place = places[k_lo : k_lo + window]
        allowed = (q_label[:, None] == k_label[None, :]) & (k_place[None, :] <= q_place[:, None])
        q_block = q_seq[q_lo : q_lo + Q_ROWS].reshape(Q_ROWS, local_q, HD)
        g_block = g_seq[q_lo : q_lo + Q_ROWS].reshape(Q_ROWS, local_q, HD)
        attn_block, dq_block, grad_k, grad_v = block_pass(
            q_block,
            g_block,
            k_all[k_lo : k_lo + window],
            v_all[k_lo : k_lo + window],
            allowed,
            score_scale,
        )
        attn_parts.append(attn_block.reshape(Q_ROWS, local_q * HD))
        dq_parts.append(dq_block.reshape(Q_ROWS, local_q * HD))
        grad_k_all = grad_k_all.at[k_lo : k_lo + window].add(grad_k)
        grad_v_all = grad_v_all.at[k_lo : k_lo + window].add(grad_v)
    grad_kv_all = jnp.concatenate([grad_k_all, grad_v_all], axis=1)
    half = span_rows // 2
    low_rows = jnp.stack(
        [grad_kv_all[g * span_rows : g * span_rows + half] for g in range(reach_groups)]
    )
    high_rows = jnp.stack(
        [grad_kv_all[g * span_rows + half : (g + 1) * span_rows] for g in range(reach_groups)]
    )
    mine_part = jnp.where(core == 0, low_rows, high_rows)
    their_part = jnp.where(core == 0, high_rows, low_rows)
    pair_sum = mine_part + lax.ppermute(their_part, "sp", sibling)
    backs = [
        passed_along(pair_sum[reach_groups - d].astype(jnp.bfloat16), "fsdp", -d)
        for d in range(1, reach_groups + 1)
    ]
    attn_seq = jnp.concatenate(attn_parts, axis=0)
    dq_seq = jnp.concatenate(dq_parts, axis=0)
    own_sum = grad_kv_all[own_start:]
    own_sum = jnp.concatenate([own_sum[:, :HD] * score_scale, own_sum[:, HD:]], axis=1)
    outgoing = jnp.concatenate([attn_seq, dq_seq, own_sum.astype(jnp.bfloat16)], axis=1)
    back_all = lax.all_to_all(outgoing, "sp", split_axis=0, concat_axis=1, tiled=True)
    back_all = back_all.reshape(tok_dev, seq_width, outgoing.shape[1])
    attn_out = back_all[:, :, :q_width].reshape(tok_dev, heads_q * HD)
    grad_queries = back_all[:, :, q_width : 2 * q_width].reshape(tok_dev, heads_q * HD)
    back_half = backs[0].astype(jnp.float32)
    for back in backs[1:]:
        back_half = back_half + back
    back_half = jnp.concatenate([back_half[:, :HD] * score_scale, back_half[:, HD:]], axis=1)
    back_full = lax.dynamic_update_slice_in_dim(
        jnp.zeros((span_rows, 2 * HD), jnp.bfloat16), back_half.astype(jnp.bfloat16), core * half, 0
    )
    kv_back = lax.all_to_all(back_full, "sp", split_axis=0, concat_axis=1, tiled=True)
    kv_back = kv_back.reshape(tok_dev, seq_width, 2 * HD).astype(jnp.float32)
    kv_back = kv_back + back_all[:, :, 2 * q_width :].astype(jnp.float32)
    kv_back = jnp.sum(kv_back.reshape(tok_dev, heads_k, seq_width // heads_k, 2 * HD), axis=2)
    grad_keys = kv_back[:, :, :HD].reshape(tok_dev, heads_k * HD)
    grad_values = kv_back[:, :, HD:].reshape(tok_dev, heads_k * HD)
    return (
        attn_out,
        grad_queries,
        grad_keys.astype(jnp.bfloat16),
        grad_values.astype(jnp.bfloat16),
    )


def solution(mesh):
    in_specs = (
        P(("fsdp", "sp"), None),
        P(("fsdp", "sp"), None),
        P(("fsdp", "sp"), None),
        P(("fsdp", "sp"), None),
        P(),
    )
    out_specs = (
        P(("fsdp", "sp"), None),
        P(("fsdp", "sp"), None),
        P(("fsdp", "sp"), None),
        P(("fsdp", "sp"), None),
    )
    return jax.shard_map(local, mesh=mesh, in_specs=in_specs, out_specs=out_specs, check_vma=False)
```

```python
import math

import jax
import jax.numpy as jnp
from jax import lax
from jax.sharding import PartitionSpec as P

HD = 128
BLK = 128
MOST_BLK = 16
Q_ROWS = 128


MASK_FILL = -1e30


def passed_along(value, axis, steps):
    count = lax.axis_size(axis)
    first, last = (max(0, -steps), min(count, count - steps))
    return lax.ppermute(value, axis, [(source, source + steps) for source in range(first, last)])


def lifted(row_data):
    return lax.optimization_barrier(row_data).astype(jnp.float32)


def doc_index(doc_lengths, first_place, row_count):
    doc_ends = jnp.cumsum(doc_lengths) * BLK
    places = first_place + jnp.arange(row_count, dtype=jnp.int32)
    labels = jnp.sum((places[:, None] >= doc_ends[None, :]).astype(jnp.int32), axis=1)
    return jnp.where(places < 0, -1, labels)


def widen_heads(row_data, copies):
    tokens_here = row_data.shape[0]
    head_count = row_data.shape[1] // HD
    shaped = row_data.reshape(tokens_here, head_count, 1, HD)
    shaped = jnp.broadcast_to(shaped, (tokens_here, head_count, copies, HD))
    return shaped.reshape(tokens_here, head_count * copies * HD)


def block_pass(q_block, g_block, k_win, v_win, allowed, score_scale):
    scores = (
        jnp.einsum("qhd,kd->hqk", q_block, k_win, preferred_element_type=jnp.float32)
        * score_scale
    )
    scores = jnp.where(allowed[None], scores, MASK_FILL)
    highest = jnp.max(scores, axis=-1, keepdims=True)
    row_total = jnp.sum(jnp.exp(scores - highest), axis=-1, keepdims=True)
    log_total = highest + jnp.log(row_total)
    weights = jnp.exp(scores - log_total)
    probs_bf = weights.astype(jnp.bfloat16)
    attn_block = jnp.einsum(
        "hqk,kd->qhd", probs_bf, v_win, preferred_element_type=jnp.float32
    ).astype(jnp.bfloat16)
    row_delta = jnp.transpose(jnp.sum(lifted(g_block) * lifted(attn_block), axis=-1), (1, 0))
    dprobs = jnp.einsum("qhd,kd->hqk", g_block, v_win, preferred_element_type=jnp.float32)
    dscores = (weights * (dprobs - row_delta[..., None])).astype(jnp.bfloat16)
    dq_block = (
        jnp.einsum("hqk,kd->qhd", dscores, k_win, preferred_element_type=jnp.float32)
        * score_scale
    ).astype(jnp.bfloat16)
    grad_k = jnp.einsum("hqk,qhd->kd", dscores, q_block, preferred_element_type=jnp.float32)
    grad_v = jnp.einsum("hqk,qhd->kd", probs_bf, g_block, preferred_element_type=jnp.float32)
    return attn_block, dq_block, grad_k, grad_v


def local(queries, key_rows, value_rows, out_grad, doc_lengths):
    seq_width = lax.axis_size("sp")
    tok_dev = queries.shape[0]
    span_rows = tok_dev * seq_width
    heads_q = queries.shape[1] // HD
    heads_k = key_rows.shape[1] // HD
    local_q = heads_q // seq_width
    copies = seq_width // heads_k
    score_scale = 1.0 / math.sqrt(HD)
    core = lax.axis_index("sp") % 2
    sibling = [(s, s ^ 1) for s in range(seq_width)]
    part_rows = tok_dev // 2
    kv_heads = jnp.concatenate(
        [key_rows.reshape(tok_dev, heads_k, HD), value_rows.reshape(tok_dev, heads_k, HD)],
        axis=2,
    )
    kv_send = jnp.transpose(kv_heads.reshape(2, part_rows, heads_k, 2 * HD), (2, 0, 1, 3))
    kv_send = kv_send.reshape(seq_width, part_rows, 2 * HD)
    kv_mine = lax.all_to_all(kv_send, "sp", split_axis=0, concat_axis=0, tiled=True)

    def joined(mine, theirs):
        return jnp.where(
            core == 0, jnp.stack([mine, theirs], axis=1), jnp.stack([theirs, mine], axis=1)
        ).reshape(span_rows, 2 * HD)

    q_width = local_q * HD
    qg_pack = jnp.concatenate(
        [
            queries.reshape(tok_dev, seq_width, q_width),
            out_grad.reshape(tok_dev, seq_width, q_width),
        ],
        axis=2,
    )
    qg_seq = lax.all_to_all(qg_pack, "sp", split_axis=1, concat_axis=0, tiled=True)
    qg_seq = qg_seq.reshape(span_rows, 2 * q_width)
    q_seq = qg_seq[:, :q_width]
    g_seq = qg_seq[:, q_width:]
    reach = MOST_BLK * BLK
    reach_groups = (reach - 1) // span_rows + 1
    first_place = lax.axis_index("fsdp") * span_rows
    received = [passed_along(kv_mine, "fsdp", d) for d in range(reach_groups, 0, -1)]
    own_theirs = lax.ppermute(kv_mine, "sp", sibling)
    swapped = lax.ppermute(jnp.stack(received), "sp", sibling)
    earlier = [joined(mine, swapped[index]) for index, mine in enumerate(received)]
    kv_all = jnp.concatenate(earlier + [joined(kv_mine, own_theirs)], axis=0)
    k_all = kv_all[:, :HD]
    v_all = kv_all[:, HD:]
    base_place = first_place - reach_groups * span_rows
    key_count = (reach_groups + 1) * span_rows
    labels = doc_index(doc_lengths, base_place, key_count)
    places = base_place + jnp.arange(key_count, dtype=jnp.int32)
    window = reach + Q_ROWS
    own_start = reach_groups * span_rows
    grad_k_all = jnp.zeros((key_count, HD), jnp.float32)
    grad_v_all = jnp.zeros((key_count, HD), jnp.float32)
    attn_parts, dq_parts = [], []
    for block in range(span_rows // Q_ROWS):
        q_lo = block * Q_ROWS
        k_lo = own_start + q_lo + Q_ROWS - window
        q_label = labels[own_start + q_lo : own_start + q_lo + Q_ROWS]
        q_place = places[own_start + q_lo : own_start + q_lo + Q_ROWS]
        k_label = labels[k_lo : k_lo + window]
        k_place = places[k_lo : k_lo + window]
        allowed = (q_label[:, None] == k_label[None, :]) & (k_place[None, :] <= q_place[:, None])
        q_block = q_seq[q_lo : q_lo + Q_ROWS].reshape(Q_ROWS, local_q, HD)
        g_block = g_seq[q_lo : q_lo + Q_ROWS].reshape(Q_ROWS, local_q, HD)
        attn_block, dq_block, grad_k, grad_v = block_pass(
            q_block,
            g_block,
            k_all[k_lo : k_lo + window],
            v_all[k_lo : k_lo + window],
            allowed,
            score_scale,
        )
        attn_parts.append(attn_block.reshape(Q_ROWS, local_q * HD))
        dq_parts.append(dq_block.reshape(Q_ROWS, local_q * HD))
        grad_k_all = grad_k_all.at[k_lo : k_lo + window].add(grad_k)
        grad_v_all = grad_v_all.at[k_lo : k_lo + window].add(grad_v)
    grad_kv_all = jnp.concatenate([grad_k_all, grad_v_all], axis=1)
    half = span_rows // 2
    low_rows = jnp.stack(
        [grad_kv_all[g * span_rows : g * span_rows + half] for g in range(reach_groups)]
    )
    high_rows = jnp.stack(
        [grad_kv_all[g * span_rows + half : (g + 1) * span_rows] for g in range(reach_groups)]
    )
    mine_part = jnp.where(core == 0, low_rows, high_rows)
    their_part = jnp.where(core == 0, high_rows, low_rows)
    pair_sum = mine_part + lax.ppermute(their_part, "sp", sibling)
    backs = [
        passed_along(pair_sum[reach_groups - d].astype(jnp.bfloat16), "fsdp", -d)
        for d in range(1, reach_groups + 1)
    ]
    attn_seq = jnp.concatenate(attn_parts, axis=0)
    dq_seq = jnp.concatenate(dq_parts, axis=0)
    outgoing = jnp.concatenate([attn_seq, dq_seq], axis=1)
    back_all = lax.all_to_all(outgoing, "sp", split_axis=0, concat_axis=1, tiled=True)
    back_all = back_all.reshape(tok_dev, seq_width, outgoing.shape[1])
    attn_out = back_all[:, :, :q_width].reshape(tok_dev, heads_q * HD)
    grad_queries = back_all[:, :, q_width:].reshape(tok_dev, heads_q * HD)
    back_half = backs[0].astype(jnp.float32)
    for back in backs[1:]:
        back_half = back_half + back
    kv_sum = grad_kv_all[own_start:]
    kv_sum = lax.dynamic_update_slice_in_dim(
        kv_sum, lax.dynamic_slice_in_dim(kv_sum, core * half, half, 0) + back_half, core * half, 0
    )
    kv_sum = jnp.concatenate([kv_sum[:, :HD] * score_scale, kv_sum[:, HD:]], axis=1)
    kv_back = lax.all_to_all(
        kv_sum.astype(jnp.bfloat16), "sp", split_axis=0, concat_axis=1, tiled=True
    )
    kv_back = kv_back.reshape(tok_dev, seq_width, 2 * HD).astype(jnp.float32)
    kv_back = jnp.sum(kv_back.reshape(tok_dev, heads_k, seq_width // heads_k, 2 * HD), axis=2)
    grad_keys = kv_back[:, :, :HD].reshape(tok_dev, heads_k * HD)
    grad_values = kv_back[:, :, HD:].reshape(tok_dev, heads_k * HD)
    return (
        attn_out,
        grad_queries,
        grad_keys.astype(jnp.bfloat16),
        grad_values.astype(jnp.bfloat16),
    )


def solution(mesh):
    in_specs = (
        P(("fsdp", "sp"), None),
        P(("fsdp", "sp"), None),
        P(("fsdp", "sp"), None),
        P(("fsdp", "sp"), None),
        P(),
    )
    out_specs = (
        P(("fsdp", "sp"), None),
        P(("fsdp", "sp"), None),
        P(("fsdp", "sp"), None),
        P(("fsdp", "sp"), None),
    )
    return jax.shard_map(local, mesh=mesh, in_specs=in_specs, out_specs=out_specs, check_vma=False)
```

```python
import math

import jax
import jax.numpy as jnp
from jax import lax
from jax.sharding import PartitionSpec as P

HD = 128
BLK = 128
MOST_BLK = 16
Q_ROWS = 256


MASK_FILL = -1e30


def passed_along(value, axis, steps):
    count = lax.axis_size(axis)
    first, last = (max(0, -steps), min(count, count - steps))
    return lax.ppermute(value, axis, [(source, source + steps) for source in range(first, last)])


def lifted(row_data):
    return lax.optimization_barrier(row_data).astype(jnp.float32)


def doc_index(doc_lengths, first_place, row_count):
    doc_ends = jnp.cumsum(doc_lengths) * BLK
    places = first_place + jnp.arange(row_count, dtype=jnp.int32)
    labels = jnp.sum((places[:, None] >= doc_ends[None, :]).astype(jnp.int32), axis=1)
    return jnp.where(places < 0, -1, labels)


def widen_heads(row_data, copies):
    tokens_here = row_data.shape[0]
    head_count = row_data.shape[1] // HD
    shaped = row_data.reshape(tokens_here, head_count, 1, HD)
    shaped = jnp.broadcast_to(shaped, (tokens_here, head_count, copies, HD))
    return shaped.reshape(tokens_here, head_count * copies * HD)


def block_pass(q_block, g_block, k_win, v_win, allowed, score_scale):
    scores = (
        jnp.einsum("qhd,kd->hqk", q_block, k_win, preferred_element_type=jnp.float32)
        * score_scale
    )
    scores = jnp.where(allowed[None], scores, MASK_FILL)
    highest = jnp.max(scores, axis=-1, keepdims=True)
    row_total = jnp.sum(jnp.exp(scores - highest), axis=-1, keepdims=True)
    log_total = highest + jnp.log(row_total)
    weights = jnp.exp(scores - log_total)
    probs_bf = weights.astype(jnp.bfloat16)
    attn_block = jnp.einsum(
        "hqk,kd->qhd", probs_bf, v_win, preferred_element_type=jnp.float32
    ).astype(jnp.bfloat16)
    row_delta = jnp.transpose(jnp.sum(lifted(g_block) * lifted(attn_block), axis=-1), (1, 0))
    dprobs = jnp.einsum("qhd,kd->hqk", g_block, v_win, preferred_element_type=jnp.float32)
    dscores = (weights * (dprobs - row_delta[..., None])).astype(jnp.bfloat16)
    dq_block = (
        jnp.einsum("hqk,kd->qhd", dscores, k_win, preferred_element_type=jnp.float32)
        * score_scale
    ).astype(jnp.bfloat16)
    grad_k = jnp.einsum("hqk,qhd->kd", dscores, q_block, preferred_element_type=jnp.float32)
    grad_v = jnp.einsum("hqk,qhd->kd", probs_bf, g_block, preferred_element_type=jnp.float32)
    return attn_block, dq_block, grad_k, grad_v


def local(queries, key_rows, value_rows, out_grad, doc_lengths):
    seq_width = lax.axis_size("sp")
    tok_dev = queries.shape[0]
    span_rows = tok_dev * seq_width
    heads_q = queries.shape[1] // HD
    heads_k = key_rows.shape[1] // HD
    local_q = heads_q // seq_width
    copies = seq_width // heads_k
    score_scale = 1.0 / math.sqrt(HD)
    core = lax.axis_index("sp") % 2
    sibling = [(s, s ^ 1) for s in range(seq_width)]
    part_rows = tok_dev // 2
    kv_heads = jnp.concatenate(
        [key_rows.reshape(tok_dev, heads_k, HD), value_rows.reshape(tok_dev, heads_k, HD)],
        axis=2,
    )
    kv_send = jnp.transpose(kv_heads.reshape(2, part_rows, heads_k, 2 * HD), (2, 0, 1, 3))
    kv_send = kv_send.reshape(seq_width, part_rows, 2 * HD)
    kv_mine = lax.all_to_all(kv_send, "sp", split_axis=0, concat_axis=0, tiled=True)

    def joined(mine, theirs):
        return jnp.where(
            core == 0, jnp.stack([mine, theirs], axis=1), jnp.stack([theirs, mine], axis=1)
        ).reshape(span_rows, 2 * HD)

    q_width = local_q * HD
    qg_pack = jnp.concatenate(
        [
            queries.reshape(tok_dev, seq_width, q_width),
            out_grad.reshape(tok_dev, seq_width, q_width),
        ],
        axis=2,
    )
    qg_seq = lax.all_to_all(qg_pack, "sp", split_axis=1, concat_axis=0, tiled=True)
    qg_seq = qg_seq.reshape(span_rows, 2 * q_width)
    q_seq = qg_seq[:, :q_width]
    g_seq = qg_seq[:, q_width:]
    reach = MOST_BLK * BLK
    reach_groups = (reach - 1) // span_rows + 1
    first_place = lax.axis_index("fsdp") * span_rows
    received = [passed_along(kv_mine, "fsdp", d) for d in range(reach_groups, 0, -1)]
    own_theirs = lax.ppermute(kv_mine, "sp", sibling)
    swapped = lax.ppermute(jnp.stack(received), "sp", sibling)
    earlier = [joined(mine, swapped[index]) for index, mine in enumerate(received)]
    kv_all = jnp.concatenate(earlier + [joined(kv_mine, own_theirs)], axis=0)
    k_all = kv_all[:, :HD]
    v_all = kv_all[:, HD:]
    base_place = first_place - reach_groups * span_rows
    key_count = (reach_groups + 1) * span_rows
    labels = doc_index(doc_lengths, base_place, key_count)
    places = base_place + jnp.arange(key_count, dtype=jnp.int32)
    window = reach + Q_ROWS
    own_start = reach_groups * span_rows
    grad_k_all = jnp.zeros((key_count, HD), jnp.float32)
    grad_v_all = jnp.zeros((key_count, HD), jnp.float32)
    attn_parts, dq_parts = [], []
    for block in range(span_rows // Q_ROWS):
        q_lo = block * Q_ROWS
        k_lo = own_start + q_lo + Q_ROWS - window
        q_label = labels[own_start + q_lo : own_start + q_lo + Q_ROWS]
        q_place = places[own_start + q_lo : own_start + q_lo + Q_ROWS]
        k_label = labels[k_lo : k_lo + window]
        k_place = places[k_lo : k_lo + window]
        allowed = (q_label[:, None] == k_label[None, :]) & (k_place[None, :] <= q_place[:, None])
        q_block = q_seq[q_lo : q_lo + Q_ROWS].reshape(Q_ROWS, local_q, HD)
        g_block = g_seq[q_lo : q_lo + Q_ROWS].reshape(Q_ROWS, local_q, HD)
        attn_block, dq_block, grad_k, grad_v = block_pass(
            q_block,
            g_block,
            k_all[k_lo : k_lo + window],
            v_all[k_lo : k_lo + window],
            allowed,
            score_scale,
        )
        attn_parts.append(attn_block.reshape(Q_ROWS, local_q * HD))
        dq_parts.append(dq_block.reshape(Q_ROWS, local_q * HD))
        grad_k_all = grad_k_all.at[k_lo : k_lo + window].add(grad_k)
        grad_v_all = grad_v_all.at[k_lo : k_lo + window].add(grad_v)
    grad_kv_all = jnp.concatenate([grad_k_all, grad_v_all], axis=1)
    half = span_rows // 2
    low_rows = jnp.stack(
        [grad_kv_all[g * span_rows : g * span_rows + half] for g in range(reach_groups)]
    )
    high_rows = jnp.stack(
        [grad_kv_all[g * span_rows + half : (g + 1) * span_rows] for g in range(reach_groups)]
    )
    mine_part = jnp.where(core == 0, low_rows, high_rows)
    their_part = jnp.where(core == 0, high_rows, low_rows)
    pair_sum = mine_part + lax.ppermute(their_part.astype(jnp.bfloat16), "sp", sibling)
    backs = [
        passed_along(pair_sum[reach_groups - d].astype(jnp.bfloat16), "fsdp", -d)
        for d in range(1, reach_groups + 1)
    ]
    attn_seq = jnp.concatenate(attn_parts, axis=0)
    dq_seq = jnp.concatenate(dq_parts, axis=0)
    outgoing = jnp.concatenate([attn_seq, dq_seq], axis=1)
    back_all = lax.all_to_all(outgoing, "sp", split_axis=0, concat_axis=1, tiled=True)
    back_all = back_all.reshape(tok_dev, seq_width, outgoing.shape[1])
    attn_out = back_all[:, :, :q_width].reshape(tok_dev, heads_q * HD)
    grad_queries = back_all[:, :, q_width:].reshape(tok_dev, heads_q * HD)
    back_half = backs[0].astype(jnp.float32)
    for back in backs[1:]:
        back_half = back_half + back
    kv_sum = grad_kv_all[own_start:]
    kv_sum = lax.dynamic_update_slice_in_dim(
        kv_sum, lax.dynamic_slice_in_dim(kv_sum, core * half, half, 0) + back_half, core * half, 0
    )
    kv_sum = jnp.concatenate([kv_sum[:, :HD] * score_scale, kv_sum[:, HD:]], axis=1)
    kv_back = lax.all_to_all(
        kv_sum.astype(jnp.bfloat16), "sp", split_axis=0, concat_axis=1, tiled=True
    )
    kv_back = kv_back.reshape(tok_dev, seq_width, 2 * HD).astype(jnp.float32)
    kv_back = jnp.sum(kv_back.reshape(tok_dev, heads_k, seq_width // heads_k, 2 * HD), axis=2)
    grad_keys = kv_back[:, :, :HD].reshape(tok_dev, heads_k * HD)
    grad_values = kv_back[:, :, HD:].reshape(tok_dev, heads_k * HD)
    return (
        attn_out,
        grad_queries,
        grad_keys.astype(jnp.bfloat16),
        grad_values.astype(jnp.bfloat16),
    )


def solution(mesh):
    in_specs = (
        P(("fsdp", "sp"), None),
        P(("fsdp", "sp"), None),
        P(("fsdp", "sp"), None),
        P(("fsdp", "sp"), None),
        P(),
    )
    out_specs = (
        P(("fsdp", "sp"), None),
        P(("fsdp", "sp"), None),
        P(("fsdp", "sp"), None),
        P(("fsdp", "sp"), None),
    )
    return jax.shard_map(local, mesh=mesh, in_specs=in_specs, out_specs=out_specs, check_vma=False)
```

```python
import math

import jax
import jax.numpy as jnp
from jax import lax
from jax.sharding import PartitionSpec as P

HD = 128
BLK = 128
MOST_BLK = 16
Q_ROWS = 256


MASK_FILL = -1e30


def passed_along(value, axis, steps):
    count = lax.axis_size(axis)
    first, last = (max(0, -steps), min(count, count - steps))
    return lax.ppermute(value, axis, [(source, source + steps) for source in range(first, last)])


def lifted(row_data):
    return lax.optimization_barrier(row_data).astype(jnp.float32)


def doc_index(doc_lengths, first_place, row_count):
    doc_ends = jnp.cumsum(doc_lengths) * BLK
    places = first_place + jnp.arange(row_count, dtype=jnp.int32)
    labels = jnp.sum((places[:, None] >= doc_ends[None, :]).astype(jnp.int32), axis=1)
    return jnp.where(places < 0, -1, labels)


def widen_heads(row_data, copies):
    tokens_here = row_data.shape[0]
    head_count = row_data.shape[1] // HD
    shaped = row_data.reshape(tokens_here, head_count, 1, HD)
    shaped = jnp.broadcast_to(shaped, (tokens_here, head_count, copies, HD))
    return shaped.reshape(tokens_here, head_count * copies * HD)


def block_pass(q_block, g_block, k_win, v_win, allowed, score_scale):
    scores = (
        jnp.einsum("qhd,kd->hqk", q_block, k_win, preferred_element_type=jnp.float32)
        * score_scale
    )
    scores = jnp.where(allowed[None], scores, MASK_FILL)
    highest = jnp.max(scores, axis=-1, keepdims=True)
    row_total = jnp.sum(jnp.exp(scores - highest), axis=-1, keepdims=True)
    log_total = highest + jnp.log(row_total)
    weights = jnp.exp(scores - log_total)
    probs_bf = weights.astype(jnp.bfloat16)
    attn_block = jnp.einsum(
        "hqk,kd->qhd", probs_bf, v_win, preferred_element_type=jnp.float32
    ).astype(jnp.bfloat16)
    row_delta = jnp.transpose(jnp.sum(g_block.astype(jnp.float32) * lifted(attn_block), axis=-1), (1, 0))
    dprobs = jnp.einsum("qhd,kd->hqk", g_block, v_win, preferred_element_type=jnp.float32)
    dscores = (weights * (dprobs - row_delta[..., None])).astype(jnp.bfloat16)
    dq_block = (
        jnp.einsum("hqk,kd->qhd", dscores, k_win, preferred_element_type=jnp.float32)
        * score_scale
    ).astype(jnp.bfloat16)
    grad_k = jnp.einsum("hqk,qhd->kd", dscores, q_block, preferred_element_type=jnp.float32)
    grad_v = jnp.einsum("hqk,qhd->kd", probs_bf, g_block, preferred_element_type=jnp.float32)
    return attn_block, dq_block, grad_k, grad_v


def local(queries, key_rows, value_rows, out_grad, doc_lengths):
    seq_width = lax.axis_size("sp")
    tok_dev = queries.shape[0]
    span_rows = tok_dev * seq_width
    heads_q = queries.shape[1] // HD
    heads_k = key_rows.shape[1] // HD
    local_q = heads_q // seq_width
    copies = seq_width // heads_k
    score_scale = 1.0 / math.sqrt(HD)
    core = lax.axis_index("sp") % 2
    sibling = [(s, s ^ 1) for s in range(seq_width)]
    part_rows = tok_dev // 2
    kv_heads = jnp.concatenate(
        [key_rows.reshape(tok_dev, heads_k, HD), value_rows.reshape(tok_dev, heads_k, HD)],
        axis=2,
    )
    kv_send = jnp.transpose(kv_heads.reshape(2, part_rows, heads_k, 2 * HD), (2, 0, 1, 3))
    kv_send = kv_send.reshape(seq_width, part_rows, 2 * HD)
    kv_mine = lax.all_to_all(kv_send, "sp", split_axis=0, concat_axis=0, tiled=True)

    def joined(mine, theirs):
        return jnp.where(
            core == 0, jnp.stack([mine, theirs], axis=1), jnp.stack([theirs, mine], axis=1)
        ).reshape(span_rows, 2 * HD)

    q_width = local_q * HD
    qg_pack = jnp.concatenate(
        [
            queries.reshape(tok_dev, seq_width, q_width),
            out_grad.reshape(tok_dev, seq_width, q_width),
        ],
        axis=2,
    )
    qg_seq = lax.all_to_all(qg_pack, "sp", split_axis=1, concat_axis=0, tiled=True)
    qg_seq = qg_seq.reshape(span_rows, 2 * q_width)
    q_seq = qg_seq[:, :q_width]
    g_seq = qg_seq[:, q_width:]
    reach = MOST_BLK * BLK
    reach_groups = (reach - 1) // span_rows + 1
    first_place = lax.axis_index("fsdp") * span_rows
    received = [passed_along(kv_mine, "fsdp", d) for d in range(reach_groups, 0, -1)]
    own_theirs = lax.ppermute(kv_mine, "sp", sibling)
    swapped = lax.ppermute(jnp.stack(received), "sp", sibling)
    earlier = [joined(mine, swapped[index]) for index, mine in enumerate(received)]
    kv_all = jnp.concatenate(earlier + [joined(kv_mine, own_theirs)], axis=0)
    k_all = kv_all[:, :HD]
    v_all = kv_all[:, HD:]
    base_place = first_place - reach_groups * span_rows
    key_count = (reach_groups + 1) * span_rows
    labels = doc_index(doc_lengths, base_place, key_count)
    places = base_place + jnp.arange(key_count, dtype=jnp.int32)
    window = reach + Q_ROWS
    own_start = reach_groups * span_rows
    grad_k_all = jnp.zeros((key_count, HD), jnp.float32)
    grad_v_all = jnp.zeros((key_count, HD), jnp.float32)
    attn_parts, dq_parts = [], []
    for block in range(span_rows // Q_ROWS):
        q_lo = block * Q_ROWS
        k_lo = own_start + q_lo + Q_ROWS - window
        q_label = labels[own_start + q_lo : own_start + q_lo + Q_ROWS]
        q_place = places[own_start + q_lo : own_start + q_lo + Q_ROWS]
        k_label = labels[k_lo : k_lo + window]
        k_place = places[k_lo : k_lo + window]
        allowed = (q_label[:, None] == k_label[None, :]) & (k_place[None, :] <= q_place[:, None])
        q_block = q_seq[q_lo : q_lo + Q_ROWS].reshape(Q_ROWS, local_q, HD)
        g_block = g_seq[q_lo : q_lo + Q_ROWS].reshape(Q_ROWS, local_q, HD)
        attn_block, dq_block, grad_k, grad_v = block_pass(
            q_block,
            g_block,
            k_all[k_lo : k_lo + window],
            v_all[k_lo : k_lo + window],
            allowed,
            score_scale,
        )
        attn_parts.append(attn_block.reshape(Q_ROWS, local_q * HD))
        dq_parts.append(dq_block.reshape(Q_ROWS, local_q * HD))
        grad_k_all = grad_k_all.at[k_lo : k_lo + window].add(grad_k)
        grad_v_all = grad_v_all.at[k_lo : k_lo + window].add(grad_v)
    grad_kv_all = jnp.concatenate([grad_k_all, grad_v_all], axis=1)
    half = span_rows // 2
    low_rows = jnp.stack(
        [grad_kv_all[g * span_rows : g * span_rows + half] for g in range(reach_groups)]
    )
    high_rows = jnp.stack(
        [grad_kv_all[g * span_rows + half : (g + 1) * span_rows] for g in range(reach_groups)]
    )
    mine_part = jnp.where(core == 0, low_rows, high_rows)
    their_part = jnp.where(core == 0, high_rows, low_rows)
    pair_sum = mine_part + lax.ppermute(their_part, "sp", sibling)
    backs = [
        passed_along(pair_sum[reach_groups - d].astype(jnp.bfloat16), "fsdp", -d)
        for d in range(1, reach_groups + 1)
    ]
    attn_seq = jnp.concatenate(attn_parts, axis=0)
    dq_seq = jnp.concatenate(dq_parts, axis=0)
    outgoing = jnp.concatenate([attn_seq, dq_seq], axis=1)
    back_all = lax.all_to_all(outgoing, "sp", split_axis=0, concat_axis=1, tiled=True)
    back_all = back_all.reshape(tok_dev, seq_width, outgoing.shape[1])
    attn_out = back_all[:, :, :q_width].reshape(tok_dev, heads_q * HD)
    grad_queries = back_all[:, :, q_width:].reshape(tok_dev, heads_q * HD)
    back_half = backs[0].astype(jnp.float32)
    for back in backs[1:]:
        back_half = back_half + back
    kv_sum = grad_kv_all[own_start:]
    kv_sum = lax.dynamic_update_slice_in_dim(
        kv_sum, lax.dynamic_slice_in_dim(kv_sum, core * half, half, 0) + back_half, core * half, 0
    )
    kv_sum = jnp.concatenate([kv_sum[:, :HD] * score_scale, kv_sum[:, HD:]], axis=1)
    kv_back = lax.all_to_all(
        kv_sum.astype(jnp.bfloat16), "sp", split_axis=0, concat_axis=1, tiled=True
    )
    kv_back = kv_back.reshape(tok_dev, seq_width, 2 * HD).astype(jnp.float32)
    kv_back = jnp.sum(kv_back.reshape(tok_dev, heads_k, seq_width // heads_k, 2 * HD), axis=2)
    grad_keys = kv_back[:, :, :HD].reshape(tok_dev, heads_k * HD)
    grad_values = kv_back[:, :, HD:].reshape(tok_dev, heads_k * HD)
    return (
        attn_out,
        grad_queries,
        grad_keys.astype(jnp.bfloat16),
        grad_values.astype(jnp.bfloat16),
    )


def solution(mesh):
    in_specs = (
        P(("fsdp", "sp"), None),
        P(("fsdp", "sp"), None),
        P(("fsdp", "sp"), None),
        P(("fsdp", "sp"), None),
        P(),
    )
    out_specs = (
        P(("fsdp", "sp"), None),
        P(("fsdp", "sp"), None),
        P(("fsdp", "sp"), None),
        P(("fsdp", "sp"), None),
    )
    return jax.shard_map(local, mesh=mesh, in_specs=in_specs, out_specs=out_specs, check_vma=False)
```
